1024 devices in a mesh: gx: 32 (over y, x, core), gy: 32 (over z).
Axes of the slice: x: 4, y: 4, z: 32, core: 2. Of those that a mesh axis runs over, the one named last changes fastest.
Arguments:
- velocity: float32 [3, 256, 256, 128], P(None, 'gx', 'gy'), may hold values from -6 to 6
- stress: float32 [6, 256, 256, 128], P(None, 'gx', 'gy'), may hold values from -6 to 6
- buoyancy: float32 [256, 256, 128], P('gx', 'gy'), may hold values from 0.25 to 0.5
- lame_lambda: float32 [256, 256, 128], P('gx', 'gy'), may hold values from 0.05 to 0.2
- lame_mu: float32 [256, 256, 128], P('gx', 'gy'), may hold values from 0.1 to 0.25
- rate_exponent: int32 [32, 32], P('gx', 'gy'), may hold values from 0 to 2
Outputs:
- velocity_out: float32 [3, 256, 256, 128], P(None, 'gx', 'gy')
- stress_out: float32 [6, 256, 256, 128], P(None, 'gx', 'gy')
The draws below stay inside these ranges and needn't reach their ends.
All inputs are finite; a program needn't handle non-finite values.
Results may differ from the reference program's by a relative error of at most 0.00002.
Values sent between devices are 32-bit elements; how exact they have to be, the bound alone decides.
No kernel may reach another device: no remote copies, remote signals or barrier semaphores. Data moves between devices by JAX's collectives and lax.ppermute only.
A program may use at most 32 MiB of HBM per device.

```python
import math
import jax
import jax.numpy as jnp

CZ = 128
TILE = 8
COARSE = 2
NX = 256
NY = 256


def set_ends(result, key, smallest, largest):
    spot = [jax.random.randint(jax.random.fold_in(key, axis), (), 0, length) for axis, length in enumerate(result.shape)]
    widest = result.shape.index(max(result.shape))
    beside = spot[:widest] + [(spot[widest] + 1) % result.shape[widest]] + spot[widest + 1:]
    return result.at[tuple(spot)].set(smallest).at[tuple(beside)].set(largest)


def shard_levels(own_key, dims, cuts, smallest, top_value):
    def one(dim, shards_of):
        steps = jax.random.uniform(jax.random.fold_in(jax.random.fold_in(own_key, 6), dim), (shards_of,), jnp.float32, smallest / len(cuts), top_value / len(cuts))
        return jnp.repeat(jnp.exp(steps), dims[dim] // shards_of).reshape((-1,) + (1,) * (len(dims) - dim - 1))

    gain = one(*cuts[0])
    for cut in cuts[1:]:
        gain = gain * one(*cut)
    return gain


def gaussian(own_key, shape, deviation, bound, pieces=(), held_as=jnp.bfloat16):
    values = jax.random.normal(own_key, shape, jnp.float32) * deviation
    if len(pieces) > 0:
        values = shard_levels(own_key, shape, pieces, -0.22, 0.18) * values
    return jnp.clip(values, min=-bound, max=bound).astype(held_as)


def setup_inputs(seed: int = 0) -> dict:
    key_of = jax.random.split(jax.random.key(seed), 7)
    return {
        "velocity": gaussian(key_of[0], (3, NX, NY, CZ), 1.0, 6.0, ((1, 32), (2, 32)), jnp.float32),
        "stress": gaussian(key_of[1], (6, NX, NY, CZ), 1.0, 6.0, ((1, 32), (2, 32)), jnp.float32),
        "buoyancy": jnp.clip(jnp.exp(math.log(0.5) - 0.6931472 * jax.random.uniform(key_of[2], (NX, NY, CZ), jnp.float32) ** shard_levels(key_of[2], (NX, NY, CZ), ((0, 32), (1, 32)), -0.2, 0.2)), 0.25, 0.5),
        "lame_lambda": jnp.clip(jnp.exp(math.log(0.2) - 1.3862944 * jax.random.uniform(key_of[3], (NX, NY, CZ), jnp.float32) ** shard_levels(key_of[3], (NX, NY, CZ), ((0, 32), (1, 32)), -0.2, 0.2)), 0.05, 0.2),
        "lame_mu": jnp.clip(jnp.exp(math.log(0.25) - 0.9162907 * jax.random.uniform(key_of[4], (NX, NY, CZ), jnp.float32) ** shard_levels(key_of[4], (NX, NY, CZ), ((0, 32), (1, 32)), -0.2, 0.2)), 0.1, 0.25),
        "rate_exponent": set_ends(jax.random.randint(key_of[5], (NX // TILE, NY // TILE), 0, 3), jax.random.fold_in(key_of[5], 1), 0, 2).astype(jnp.int32),
    }


def expand_levels(rate_exponent):
    cells = jnp.repeat(jnp.repeat(rate_exponent, TILE, axis=0), TILE, axis=1)
    return cells[:, :, None]


def level_scale(exponent):
    return jnp.where(exponent == 2, 0.25, jnp.where(exponent == 1, 0.5, 1.0)).astype(jnp.float32)


def substep_active(exponent, sub):
    odd_sub = sub % 2 == 1
    last_sub = sub == 3
    return (exponent == 2) | ((exponent == 1) & odd_sub) | ((exponent >= 0) & last_sub)


def centre(field):
    return field[1:-1, 1:-1]


def plus_x(field):
    return field[2:, 1:-1]


def minus_x(field):
    return field[:-2, 1:-1]


def plus_y(field):
    return field[1:-1, 2:]


def minus_y(field):
    return field[1:-1, :-2]


def z_forward(field):
    return jnp.concatenate([field[..., 1:], jnp.zeros_like(field[..., :1])], axis=-1) - field


def z_backward(field):
    return field - jnp.concatenate([jnp.zeros_like(field[..., :1]), field[..., :-1]], axis=-1)


def velocity_forces(padded, stress_zz):
    stress_xx, stress_yy, stress_xy, stress_xz, stress_yz = padded[0], padded[1], padded[2], padded[3], padded[4]
    force_x = (plus_x(stress_xx) - centre(stress_xx)) + (centre(stress_xy) - minus_y(stress_xy)) + z_backward(centre(stress_xz))
    force_y = (centre(stress_xy) - minus_x(stress_xy)) + (plus_y(stress_yy) - centre(stress_yy)) + z_backward(centre(stress_yz))
    force_z = (centre(stress_xz) - minus_x(stress_xz)) + (centre(stress_yz) - minus_y(stress_yz)) + z_forward(stress_zz)
    return jnp.stack([force_x, force_y, force_z])


def advance_velocity(velocity, forces, push_coef, active):
    return jnp.where(active, velocity + push_coef * forces, velocity)


def advance_stress(stress, vel_padded, lam_coef, shear_coef, active):
    vel_x, vel_y, vel_z = vel_padded[0], vel_padded[1], vel_padded[2]
    strain_x = centre(vel_x) - minus_x(vel_x)
    strain_y = centre(vel_y) - minus_y(vel_y)
    strain_z = z_backward(centre(vel_z))
    shear_xy = (plus_y(vel_x) - centre(vel_x)) + (plus_x(vel_y) - centre(vel_y))
    shear_xz = z_forward(centre(vel_x)) + (plus_x(vel_z) - centre(vel_z))
    shear_yz = z_forward(centre(vel_y)) + (plus_y(vel_z) - centre(vel_z))
    trace_sum = strain_x + strain_y + strain_z
    two_shear = 2.0 * shear_coef
    fresh = jnp.stack([
        stress[0] + (lam_coef * trace_sum + two_shear * strain_x),
        stress[1] + (lam_coef * trace_sum + two_shear * strain_y),
        stress[2] + shear_coef * shear_xy,
        stress[3] + shear_coef * shear_xz,
        stress[4] + shear_coef * shear_yz,
        stress[5] + (lam_coef * trace_sum + two_shear * strain_z),
    ])
    return jnp.where(active, fresh, stress)


def reference(velocity, stress, buoyancy, lame_lambda, lame_mu, rate_exponent):
    exponent = expand_levels(rate_exponent)
    scale = level_scale(exponent)
    push_coef = buoyancy * scale
    lam_coef = lame_lambda * scale
    shear_coef = lame_mu * scale
    widths = ((0, 0), (1, 1), (1, 1), (0, 0))
    for step in range(COARSE):
        for sub in range(4):
            active = substep_active(exponent, sub)
            padded = jnp.pad(stress[:5], widths)
            velocity = advance_velocity(velocity, velocity_forces(padded, stress[5]), push_coef, active)
            vel_padded = jnp.pad(velocity, widths)
            stress = advance_stress(stress, vel_padded, lam_coef, shear_coef, active)
    return velocity, stress
```

```python
import jax
import jax.numpy as jnp
from jax import lax
from jax.sharding import PartitionSpec as P

TILE = 8
COARSE = 2
SUBSTEPS = 4


def level_scale(exponent):
    return jnp.where(exponent == 2, 0.25, jnp.where(exponent == 1, 0.5, 1.0)).astype(jnp.float32)


def centre(field):
    return field[1:-1, 1:-1]


def plus_x(field):
    return field[2:, 1:-1]


def minus_x(field):
    return field[:-2, 1:-1]


def plus_y(field):
    return field[1:-1, 2:]


def minus_y(field):
    return field[1:-1, :-2]


def z_forward(field):
    return jnp.concatenate([field[..., 1:], jnp.zeros_like(field[..., :1])], axis=-1) - field


def z_backward(field):
    return field - jnp.concatenate([jnp.zeros_like(field[..., :1]), field[..., :-1]], axis=-1)


def velocity_forces(padded, stress_zz):
    stress_xx, stress_yy, stress_xy, stress_xz, stress_yz = (
        padded[0],
        padded[1],
        padded[2],
        padded[3],
        padded[4],
    )
    force_x = (
        plus_x(stress_xx)
        - centre(stress_xx)
        + (centre(stress_xy) - minus_y(stress_xy))
        + z_backward(centre(stress_xz))
    )
    force_y = (
        centre(stress_xy)
        - minus_x(stress_xy)
        + (plus_y(stress_yy) - centre(stress_yy))
        + z_backward(centre(stress_yz))
    )
    force_z = (
        centre(stress_xz)
        - minus_x(stress_xz)
        + (centre(stress_yz) - minus_y(stress_yz))
        + z_forward(stress_zz)
    )
    return jnp.stack([force_x, force_y, force_z])


def advance_velocity(velocity, forces, push_coef, active):
    fresh = velocity + push_coef * forces
    if active is None:
        return fresh
    return jnp.where(active, fresh, velocity)


def advance_stress(stress, vel_padded, lam_coef, shear_coef, active):
    vel_x, vel_y, vel_z = (vel_padded[0], vel_padded[1], vel_padded[2])
    strain_x = centre(vel_x) - minus_x(vel_x)
    strain_y = centre(vel_y) - minus_y(vel_y)
    strain_z = z_backward(centre(vel_z))
    shear_xy = plus_y(vel_x) - centre(vel_x) + (plus_x(vel_y) - centre(vel_y))
    shear_xz = z_forward(centre(vel_x)) + (plus_x(vel_z) - centre(vel_z))
    shear_yz = z_forward(centre(vel_y)) + (plus_y(vel_z) - centre(vel_z))
    trace_sum = strain_x + strain_y + strain_z
    two_shear = 2.0 * shear_coef
    fresh = jnp.stack(
        [
            stress[0] + (lam_coef * trace_sum + two_shear * strain_x),
            stress[1] + (lam_coef * trace_sum + two_shear * strain_y),
            stress[2] + shear_coef * shear_xy,
            stress[3] + shear_coef * shear_xz,
            stress[4] + shear_coef * shear_yz,
            stress[5] + (lam_coef * trace_sum + two_shear * strain_z),
        ]
    )
    if active is None:
        return fresh
    return jnp.where(active, fresh, stress)


def with_blocks(cells, axis, dim):
    count = lax.axis_size(axis)
    from_below = lax.ppermute(cells, axis, [(i, i + 1) for i in range(count - 1)])
    from_above = lax.ppermute(cells, axis, [(i + 1, i) for i in range(count - 1)])
    return jnp.concatenate([from_below, cells, from_above], axis=dim)


def per_device(velocity, stress, buoyancy, lame_lambda, lame_mu, rate_exponent):
    nx, ny = velocity.shape[1], velocity.shape[2]
    exponent = rate_exponent[0, 0]
    scale = level_scale(exponent)
    level = jnp.full(buoyancy.shape, exponent.astype(jnp.float32))
    block = jnp.concatenate(
        [
            velocity,
            stress,
            (buoyancy * scale)[None],
            (lame_lambda * scale)[None],
            (lame_mu * scale)[None],
            level[None],
        ],
        axis=0,
    )
    block = with_blocks(block, "gx", 1)
    block = with_blocks(block, "gy", 2)
    vel = block[0:3]
    strs = block[3:9]
    push, lam, shear, lvl = block[9], block[10], block[11], block[12]
    widths = ((0, 0), (1, 1), (1, 1), (0, 0))
    for step in range(COARSE):
        for sub in range(SUBSTEPS):
            if sub == 3:
                active = None
            elif sub == 1:
                active = lvl >= 1.0
            else:
                active = lvl == 2.0
            padded = jnp.pad(strs[:5], widths)
            vel = advance_velocity(vel, velocity_forces(padded, strs[5]), push, active)
            vel_padded = jnp.pad(vel, widths)
            strs = advance_stress(strs, vel_padded, lam, shear, active)
            vel = vel[:, 1:-1]
            strs = strs[:, 1:-1]
            push, lam, shear, lvl = push[1:-1], lam[1:-1], shear[1:-1], lvl[1:-1]
    vel = vel[:, :, ny : 2 * ny]
    strs = strs[:, :, ny : 2 * ny]
    return (vel, strs)


def solution(mesh):
    in_specs = (
        P(None, "gx", "gy", None),
        P(None, "gx", "gy", None),
        P("gx", "gy", None),
        P("gx", "gy", None),
        P("gx", "gy", None),
        P("gx", "gy"),
    )
    out_specs = (P(None, "gx", "gy", None), P(None, "gx", "gy", None))
    return jax.shard_map(
        per_device, mesh=mesh, in_specs=in_specs, out_specs=out_specs, check_vma=False
    )
```

```python
import jax
import jax.numpy as jnp
from jax import lax
from jax.sharding import PartitionSpec as P

TILE = 8
COARSE = 2
SUBSTEPS = 4


def level_scale(exponent):
    return jnp.where(exponent == 2, 0.25, jnp.where(exponent == 1, 0.5, 1.0)).astype(jnp.float32)


def centre(field):
    return field[1:-1, 1:-1]


def plus_x(field):
    return field[2:, 1:-1]


def minus_x(field):
    return field[:-2, 1:-1]


def plus_y(field):
    return field[1:-1, 2:]


def minus_y(field):
    return field[1:-1, :-2]


def z_forward(field):
    return jnp.concatenate([field[..., 1:], jnp.zeros_like(field[..., :1])], axis=-1) - field


def z_backward(field):
    return field - jnp.concatenate([jnp.zeros_like(field[..., :1]), field[..., :-1]], axis=-1)


def velocity_forces(padded, stress_zz):
    stress_xx, stress_yy, stress_xy, stress_xz, stress_yz = (
        padded[0],
        padded[1],
        padded[2],
        padded[3],
        padded[4],
    )
    force_x = (
        plus_x(stress_xx)
        - centre(stress_xx)
        + (centre(stress_xy) - minus_y(stress_xy))
        + z_backward(centre(stress_xz))
    )
    force_y = (
        centre(stress_xy)
        - minus_x(stress_xy)
        + (plus_y(stress_yy) - centre(stress_yy))
        + z_backward(centre(stress_yz))
    )
    force_z = (
        centre(stress_xz)
        - minus_x(stress_xz)
        + (centre(stress_yz) - minus_y(stress_yz))
        + z_forward(stress_zz)
    )
    return jnp.stack([force_x, force_y, force_z])


def advance_velocity(velocity, forces, push_coef, active):
    fresh = velocity + push_coef * forces
    if active is None:
        return fresh
    return jnp.where(active, fresh, velocity)


def advance_stress(stress, vel_padded, lam_coef, shear_coef, active):
    vel_x, vel_y, vel_z = (vel_padded[0], vel_padded[1], vel_padded[2])
    strain_x = centre(vel_x) - minus_x(vel_x)
    strain_y = centre(vel_y) - minus_y(vel_y)
    strain_z = z_backward(centre(vel_z))
    shear_xy = plus_y(vel_x) - centre(vel_x) + (plus_x(vel_y) - centre(vel_y))
    shear_xz = z_forward(centre(vel_x)) + (plus_x(vel_z) - centre(vel_z))
    shear_yz = z_forward(centre(vel_y)) + (plus_y(vel_z) - centre(vel_z))
    trace_sum = strain_x + strain_y + strain_z
    two_shear = 2.0 * shear_coef
    fresh = jnp.stack(
        [
            stress[0] + (lam_coef * trace_sum + two_shear * strain_x),
            stress[1] + (lam_coef * trace_sum + two_shear * strain_y),
            stress[2] + shear_coef * shear_xy,
            stress[3] + shear_coef * shear_xz,
            stress[4] + shear_coef * shear_yz,
            stress[5] + (lam_coef * trace_sum + two_shear * strain_z),
        ]
    )
    if active is None:
        return fresh
    return jnp.where(active, fresh, stress)


def with_blocks(cells, axis, dim):
    count = lax.axis_size(axis)
    from_below = lax.ppermute(cells, axis, [(i, i + 1) for i in range(count - 1)])
    from_above = lax.ppermute(cells, axis, [(i + 1, i) for i in range(count - 1)])
    return jnp.concatenate([from_below, cells, from_above], axis=dim)


def per_device(velocity, stress, buoyancy, lame_lambda, lame_mu, rate_exponent):
    nx, ny = velocity.shape[1], velocity.shape[2]
    exponent = rate_exponent[0, 0]
    scale = level_scale(exponent)
    level = jnp.full(buoyancy.shape, exponent.astype(jnp.float32))
    block = jnp.concatenate(
        [
            velocity,
            stress,
            (buoyancy * scale)[None],
            (lame_lambda * scale)[None],
            (lame_mu * scale)[None],
            level[None],
        ],
        axis=0,
    )
    block = with_blocks(block, "gy", 2)
    block = with_blocks(block, "gx", 1)
    vel = block[0:3]
    strs = block[3:9]
    push, lam, shear, lvl = block[9], block[10], block[11], block[12]
    widths = ((0, 0), (1, 1), (1, 1), (0, 0))
    for step in range(COARSE):
        for sub in range(SUBSTEPS):
            if sub == 3:
                active = None
            elif sub == 1:
                active = lvl >= 1.0
            else:
                active = lvl == 2.0
            padded = jnp.pad(strs[:5], widths)
            vel = advance_velocity(vel, velocity_forces(padded, strs[5]), push, active)
            vel_padded = jnp.pad(vel, widths)
            strs = advance_stress(strs, vel_padded, lam, shear, active)
            vel = vel[:, 1:-1]
            strs = strs[:, 1:-1]
            push, lam, shear, lvl = push[1:-1], lam[1:-1], shear[1:-1], lvl[1:-1]
    vel = vel[:, :, ny : 2 * ny]
    strs = strs[:, :, ny : 2 * ny]
    return (vel, strs)


def solution(mesh):
    in_specs = (
        P(None, "gx", "gy", None),
        P(None, "gx", "gy", None),
        P("gx", "gy", None),
        P("gx", "gy", None),
        P("gx", "gy", None),
        P("gx", "gy"),
    )
    out_specs = (P(None, "gx", "gy", None), P(None, "gx", "gy", None))
    return jax.shard_map(
        per_device, mesh=mesh, in_specs=in_specs, out_specs=out_specs, check_vma=False
    )
```

```python
import jax
import jax.numpy as jnp
from jax import lax
from jax.sharding import PartitionSpec as P
from jax.experimental import pallas as pl
from jax.experimental.pallas import tpu as pltpu

TILE = 8
COARSE = 2
SUBSTEPS = 4


def level_scale(exponent):
    return jnp.where(exponent == 2, 0.25, jnp.where(exponent == 1, 0.5, 1.0)).astype(jnp.float32)


def centre(field):
    return field[1:-1, 1:-1]


def plus_x(field):
    return field[2:, 1:-1]


def minus_x(field):
    return field[:-2, 1:-1]


def plus_y(field):
    return field[1:-1, 2:]


def minus_y(field):
    return field[1:-1, :-2]


def z_forward(field):
    return jnp.concatenate([field[..., 1:], jnp.zeros_like(field[..., :1])], axis=-1) - field


def z_backward(field):
    return field - jnp.concatenate([jnp.zeros_like(field[..., :1]), field[..., :-1]], axis=-1)


def velocity_forces(padded, stress_zz):
    stress_xx, stress_yy, stress_xy, stress_xz, stress_yz = (
        padded[0],
        padded[1],
        padded[2],
        padded[3],
        padded[4],
    )
    force_x = (
        plus_x(stress_xx)
        - centre(stress_xx)
        + (centre(stress_xy) - minus_y(stress_xy))
        + z_backward(centre(stress_xz))
    )
    force_y = (
        centre(stress_xy)
        - minus_x(stress_xy)
        + (plus_y(stress_yy) - centre(stress_yy))
        + z_backward(centre(stress_yz))
    )
    force_z = (
        centre(stress_xz)
        - minus_x(stress_xz)
        + (centre(stress_yz) - minus_y(stress_yz))
        + z_forward(stress_zz)
    )
    return jnp.stack([force_x, force_y, force_z])


def advance_velocity(velocity, forces, push_coef, active):
    fresh = velocity + push_coef * forces
    if active is None:
        return fresh
    return jnp.where(active, fresh, velocity)


def advance_stress(stress, vel_padded, lam_coef, shear_coef, active):
    vel_x, vel_y, vel_z = (vel_padded[0], vel_padded[1], vel_padded[2])
    strain_x = centre(vel_x) - minus_x(vel_x)
    strain_y = centre(vel_y) - minus_y(vel_y)
    strain_z = z_backward(centre(vel_z))
    shear_xy = plus_y(vel_x) - centre(vel_x) + (plus_x(vel_y) - centre(vel_y))
    shear_xz = z_forward(centre(vel_x)) + (plus_x(vel_z) - centre(vel_z))
    shear_yz = z_forward(centre(vel_y)) + (plus_y(vel_z) - centre(vel_z))
    trace_sum = strain_x + strain_y + strain_z
    two_shear = 2.0 * shear_coef
    fresh = jnp.stack(
        [
            stress[0] + (lam_coef * trace_sum + two_shear * strain_x),
            stress[1] + (lam_coef * trace_sum + two_shear * strain_y),
            stress[2] + shear_coef * shear_xy,
            stress[3] + shear_coef * shear_xz,
            stress[4] + shear_coef * shear_yz,
            stress[5] + (lam_coef * trace_sum + two_shear * strain_z),
        ]
    )
    if active is None:
        return fresh
    return jnp.where(active, fresh, stress)


def with_blocks(cells, axis, dim):
    count = lax.axis_size(axis)
    from_below = lax.ppermute(cells, axis, [(i, i + 1) for i in range(count - 1)])
    from_above = lax.ppermute(cells, axis, [(i + 1, i) for i in range(count - 1)])
    return jnp.concatenate([from_below, cells, from_above], axis=dim)


INTERPRET = False
YOFF = 8


def lane_shifts(shape):
    lane = lax.broadcasted_iota(jnp.int32, shape, len(shape) - 1)
    width = shape[-1]
    from_below = pltpu.roll(lane, 1, len(shape) - 1) == (lane + (width - 1)) % width
    first = lane == 0
    last = lane == width - 1
    axis = len(shape) - 1

    def z_backward(f):
        one, back = pltpu.roll(f, 1, axis), pltpu.roll(f, width - 1, axis)
        prev = jnp.where(first, 0.0, jnp.where(from_below, one, back))
        return f - prev

    def z_forward(f):
        one, back = pltpu.roll(f, 1, axis), pltpu.roll(f, width - 1, axis)
        nxt = jnp.where(last, 0.0, jnp.where(from_below, back, one))
        return nxt - f

    return z_backward, z_forward


def substeps_kernel(ext_ref, vel_out, strs_out, vbuf, sbuf):
    rows, cols, depth = ext_ref.shape[1], ext_ref.shape[2], ext_ref.shape[3]
    ny = vel_out.shape[2]
    nx = vel_out.shape[1]
    halo = (rows - nx) // 2
    pad_rows = vbuf.shape[2] - cols - YOFF
    zero_y = jnp.zeros((vbuf.shape[1], YOFF, depth), jnp.float32)
    zero_y2 = jnp.zeros((vbuf.shape[1], pad_rows, depth), jnp.float32)
    zero_x = jnp.zeros((1, vbuf.shape[2], depth), jnp.float32)
    for buf, count in ((vbuf, 3), (sbuf, 6)):
        for c in range(count):
            buf[c, :, 0:YOFF, :] = zero_y
            buf[c, :, YOFF + cols :, :] = zero_y2
            buf[c, 0:1, :, :] = zero_x
            buf[c, rows + 1 : rows + 2, :, :] = zero_x
    for c in range(3):
        vbuf[c, 1 : rows + 1, YOFF : YOFF + cols, :] = ext_ref[c]
    for c in range(6):
        sbuf[c, 1 : rows + 1, YOFF : YOFF + cols, :] = ext_ref[3 + c]
    z_backward, z_forward = lane_shifts((1, cols, depth))
    ys = pl.ds(YOFF, cols)
    ym = pl.ds(YOFF - 1, cols)
    yp = pl.ds(YOFF + 1, cols)

    def mask_of(sub, r):
        if sub == 3:
            return None
        lvl = ext_ref[12, pl.ds(r, 1), :, :]
        return lvl >= 1.0 if sub == 1 else lvl == 2.0

    def keep(active, fresh, old):
        return fresh if active is None else jnp.where(active, fresh, old)

    for step in range(COARSE):
        for sub in range(SUBSTEPS):
            t = step * SUBSTEPS + sub
            lo, hi = t + 1, rows + 1 - t

            def vel_row(b, carry, sub=sub):
                r = b - 1
                sxx_c = sbuf[0, pl.ds(b, 1), ys, :]
                sxx_px = sbuf[0, pl.ds(b + 1, 1), ys, :]
                syy_c = sbuf[1, pl.ds(b, 1), ys, :]
                syy_py = sbuf[1, pl.ds(b, 1), yp, :]
                sxy_c = sbuf[2, pl.ds(b, 1), ys, :]
                sxy_my = sbuf[2, pl.ds(b, 1), ym, :]
                sxy_mx = sbuf[2, pl.ds(b - 1, 1), ys, :]
                sxz_c = sbuf[3, pl.ds(b, 1), ys, :]
                sxz_mx = sbuf[3, pl.ds(b - 1, 1), ys, :]
                syz_c = sbuf[4, pl.ds(b, 1), ys, :]
                syz_my = sbuf[4, pl.ds(b, 1), ym, :]
                szz_c = sbuf[5, pl.ds(b, 1), ys, :]
                force_x = sxx_px - sxx_c + (sxy_c - sxy_my) + z_backward(sxz_c)
                force_y = sxy_c - sxy_mx + (syy_py - syy_c) + z_backward(syz_c)
                force_z = sxz_c - sxz_mx + (syz_c - syz_my) + z_forward(szz_c)
                push = ext_ref[9, pl.ds(r, 1), :, :]
                active = mask_of(sub, r)
                for c, force in enumerate((force_x, force_y, force_z)):
                    old = vbuf[c, pl.ds(b, 1), ys, :]
                    vbuf[c, pl.ds(b, 1), ys, :] = keep(active, old + push * force, old)
                return carry

            lax.fori_loop(lo, hi, vel_row, 0)

            def strs_row(b, carry, sub=sub):
                r = b - 1
                vx_c = vbuf[0, pl.ds(b, 1), ys, :]
                vx_mx = vbuf[0, pl.ds(b - 1, 1), ys, :]
                vx_py = vbuf[0, pl.ds(b, 1), yp, :]
                vy_c = vbuf[1, pl.ds(b, 1), ys, :]
                vy_my = vbuf[1, pl.ds(b, 1), ym, :]
                vy_px = vbuf[1, pl.ds(b + 1, 1), ys, :]
                vz_c = vbuf[2, pl.ds(b, 1), ys, :]
                vz_px = vbuf[2, pl.ds(b + 1, 1), ys, :]
                vz_py = vbuf[2, pl.ds(b, 1), yp, :]
                strain_x = vx_c - vx_mx
                strain_y = vy_c - vy_my
                strain_z = z_backward(vz_c)
                shear_xy = vx_py - vx_c + (vy_px - vy_c)
                shear_xz = z_forward(vx_c) + (vz_px - vz_c)
                shear_yz = z_forward(vy_c) + (vz_py - vz_c)
                trace_sum = strain_x + strain_y + strain_z
                lam = ext_ref[10, pl.ds(r, 1), :, :]
                shear = ext_ref[11, pl.ds(r, 1), :, :]
                two_shear = 2.0 * shear
                adds = (
                    lam * trace_sum + two_shear * strain_x,
                    lam * trace_sum + two_shear * strain_y,
                    shear * shear_xy,
                    shear * shear_xz,
                    shear * shear_yz,
                    lam * trace_sum + two_shear * strain_z,
                )
                active = mask_of(sub, r)
                for c, add in enumerate(adds):
                    old = sbuf[c, pl.ds(b, 1), ys, :]
                    sbuf[c, pl.ds(b, 1), ys, :] = keep(active, old + add, old)
                return carry

            lax.fori_loop(lo, hi, strs_row, 0)

    xs = slice(halo + 1, halo + 1 + nx)
    yc = slice(YOFF + halo, YOFF + halo + ny)
    for c in range(3):
        vel_out[c] = vbuf[c, xs, yc, :]
    for c in range(6):
        strs_out[c] = sbuf[c, xs, yc, :]


def substeps(ext, nx, ny):
    fields, rows, cols, depth = ext.shape
    return pl.pallas_call(
        substeps_kernel,
        out_shape=(
            jax.ShapeDtypeStruct((3, nx, ny, depth), jnp.float32),
            jax.ShapeDtypeStruct((6, nx, ny, depth), jnp.float32),
        ),
        scratch_shapes=[
            pltpu.VMEM((3, rows + 2, cols + 2 * YOFF, depth), jnp.float32),
            pltpu.VMEM((6, rows + 2, cols + 2 * YOFF, depth), jnp.float32),
        ],
        interpret=INTERPRET,
    )(ext)


def per_device(velocity, stress, buoyancy, lame_lambda, lame_mu, rate_exponent):
    nx, ny = velocity.shape[1], velocity.shape[2]
    exponent = rate_exponent[0, 0]
    scale = level_scale(exponent)
    level = jnp.full(buoyancy.shape, exponent.astype(jnp.float32))
    block = jnp.concatenate(
        [
            velocity,
            stress,
            (buoyancy * scale)[None],
            (lame_lambda * scale)[None],
            (lame_mu * scale)[None],
            level[None],
        ],
        axis=0,
    )
    block = with_blocks(block, "gy", 2)
    block = with_blocks(block, "gx", 1)
    return substeps(block, nx, ny)


def solution(mesh):
    in_specs = (
        P(None, "gx", "gy", None),
        P(None, "gx", "gy", None),
        P("gx", "gy", None),
        P("gx", "gy", None),
        P("gx", "gy", None),
        P("gx", "gy"),
    )
    out_specs = (P(None, "gx", "gy", None), P(None, "gx", "gy", None))
    return jax.shard_map(
        per_device, mesh=mesh, in_specs=in_specs, out_specs=out_specs, check_vma=False
    )
```

```python
import jax
import jax.numpy as jnp
from jax import lax
from jax.sharding import PartitionSpec as P
from jax.experimental import pallas as pl
from jax.experimental.pallas import tpu as pltpu

TILE = 8
COARSE = 2
SUBSTEPS = 4


def level_scale(exponent):
    return jnp.where(exponent == 2, 0.25, jnp.where(exponent == 1, 0.5, 1.0)).astype(jnp.float32)


def centre(field):
    return field[1:-1, 1:-1]


def plus_x(field):
    return field[2:, 1:-1]


def minus_x(field):
    return field[:-2, 1:-1]


def plus_y(field):
    return field[1:-1, 2:]


def minus_y(field):
    return field[1:-1, :-2]


def z_forward(field):
    return jnp.concatenate([field[..., 1:], jnp.zeros_like(field[..., :1])], axis=-1) - field


def z_backward(field):
    return field - jnp.concatenate([jnp.zeros_like(field[..., :1]), field[..., :-1]], axis=-1)


def velocity_forces(padded, stress_zz):
    stress_xx, stress_yy, stress_xy, stress_xz, stress_yz = (
        padded[0],
        padded[1],
        padded[2],
        padded[3],
        padded[4],
    )
    force_x = (
        plus_x(stress_xx)
        - centre(stress_xx)
        + (centre(stress_xy) - minus_y(stress_xy))
        + z_backward(centre(stress_xz))
    )
    force_y = (
        centre(stress_xy)
        - minus_x(stress_xy)
        + (plus_y(stress_yy) - centre(stress_yy))
        + z_backward(centre(stress_yz))
    )
    force_z = (
        centre(stress_xz)
        - minus_x(stress_xz)
        + (centre(stress_yz) - minus_y(stress_yz))
        + z_forward(stress_zz)
    )
    return jnp.stack([force_x, force_y, force_z])


def advance_velocity(velocity, forces, push_coef, active):
    fresh = velocity + push_coef * forces
    if active is None:
        return fresh
    return jnp.where(active, fresh, velocity)


def advance_stress(stress, vel_padded, lam_coef, shear_coef, active):
    vel_x, vel_y, vel_z = (vel_padded[0], vel_padded[1], vel_padded[2])
    strain_x = centre(vel_x) - minus_x(vel_x)
    strain_y = centre(vel_y) - minus_y(vel_y)
    strain_z = z_backward(centre(vel_z))
    shear_xy = plus_y(vel_x) - centre(vel_x) + (plus_x(vel_y) - centre(vel_y))
    shear_xz = z_forward(centre(vel_x)) + (plus_x(vel_z) - centre(vel_z))
    shear_yz = z_forward(centre(vel_y)) + (plus_y(vel_z) - centre(vel_z))
    trace_sum = strain_x + strain_y + strain_z
    two_shear = 2.0 * shear_coef
    fresh = jnp.stack(
        [
            stress[0] + (lam_coef * trace_sum + two_shear * strain_x),
            stress[1] + (lam_coef * trace_sum + two_shear * strain_y),
            stress[2] + shear_coef * shear_xy,
            stress[3] + shear_coef * shear_xz,
            stress[4] + shear_coef * shear_yz,
            stress[5] + (lam_coef * trace_sum + two_shear * strain_z),
        ]
    )
    if active is None:
        return fresh
    return jnp.where(active, fresh, stress)


def with_blocks(cells, axis, dim):
    count = lax.axis_size(axis)
    from_below = lax.ppermute(cells, axis, [(i, i + 1) for i in range(count - 1)])
    from_above = lax.ppermute(cells, axis, [(i + 1, i) for i in range(count - 1)])
    return jnp.concatenate([from_below, cells, from_above], axis=dim)


INTERPRET = False
YOFF = 8


def lane_shifts(shape):
    lane = lax.broadcasted_iota(jnp.int32, shape, len(shape) - 1)
    width = shape[-1]
    from_below = pltpu.roll(lane, 1, len(shape) - 1) == (lane + (width - 1)) % width
    first = lane == 0
    last = lane == width - 1
    axis = len(shape) - 1

    def z_backward(f):
        one, back = pltpu.roll(f, 1, axis), pltpu.roll(f, width - 1, axis)
        prev = jnp.where(first, 0.0, jnp.where(from_below, one, back))
        return f - prev

    def z_forward(f):
        one, back = pltpu.roll(f, 1, axis), pltpu.roll(f, width - 1, axis)
        nxt = jnp.where(last, 0.0, jnp.where(from_below, back, one))
        return nxt - f

    return z_backward, z_forward


def substeps_kernel(below_ref, mid_ref, above_ref, vel_out, strs_out, vbuf, sbuf, ext_ref):
    piece = mid_ref.shape[1]
    rows, cols, depth = 3 * piece, mid_ref.shape[2], mid_ref.shape[3]
    ny = vel_out.shape[2]
    nx = vel_out.shape[1]
    halo = (rows - nx) // 2
    pad_rows = vbuf.shape[2] - cols - YOFF
    zero_y = jnp.zeros((vbuf.shape[1], YOFF, depth), jnp.float32)
    zero_y2 = jnp.zeros((vbuf.shape[1], pad_rows, depth), jnp.float32)
    zero_x = jnp.zeros((1, vbuf.shape[2], depth), jnp.float32)
    for buf, count in ((vbuf, 3), (sbuf, 6)):
        for c in range(count):
            buf[c, :, 0:YOFF, :] = zero_y
            buf[c, :, YOFF + cols :, :] = zero_y2
            buf[c, 0:1, :, :] = zero_x
            buf[c, rows + 1 : rows + 2, :, :] = zero_x
    for k, src in enumerate((below_ref, mid_ref, above_ref)):
        at = 1 + k * piece
        for c in range(3):
            vbuf[c, at : at + piece, YOFF : YOFF + cols, :] = src[c]
        for c in range(6):
            sbuf[c, at : at + piece, YOFF : YOFF + cols, :] = src[3 + c]
        for c in range(4):
            ext_ref[9 + c, at - 1 : at - 1 + piece, :, :] = src[9 + c]
    z_backward, z_forward = lane_shifts((1, cols, depth))
    ys = pl.ds(YOFF, cols)
    ym = pl.ds(YOFF - 1, cols)
    yp = pl.ds(YOFF + 1, cols)

    def mask_of(sub, r):
        if sub == 3:
            return None
        lvl = ext_ref[12, pl.ds(r, 1), :, :]
        return lvl >= 1.0 if sub == 1 else lvl == 2.0

    def keep(active, fresh, old):
        return fresh if active is None else jnp.where(active, fresh, old)

    for step in range(COARSE):
        for sub in range(SUBSTEPS):
            t = step * SUBSTEPS + sub
            lo, hi = t + 1, rows + 1 - t

            def vel_row(b, carry, sub=sub):
                r = b - 1
                sxx_c = sbuf[0, pl.ds(b, 1), ys, :]
                sxx_px = sbuf[0, pl.ds(b + 1, 1), ys, :]
                syy_c = sbuf[1, pl.ds(b, 1), ys, :]
                syy_py = sbuf[1, pl.ds(b, 1), yp, :]
                sxy_c = sbuf[2, pl.ds(b, 1), ys, :]
                sxy_my = sbuf[2, pl.ds(b, 1), ym, :]
                sxy_mx = sbuf[2, pl.ds(b - 1, 1), ys, :]
                sxz_c = sbuf[3, pl.ds(b, 1), ys, :]
                sxz_mx = sbuf[3, pl.ds(b - 1, 1), ys, :]
                syz_c = sbuf[4, pl.ds(b, 1), ys, :]
                syz_my = sbuf[4, pl.ds(b, 1), ym, :]
                szz_c = sbuf[5, pl.ds(b, 1), ys, :]
                force_x = sxx_px - sxx_c + (sxy_c - sxy_my) + z_backward(sxz_c)
                force_y = sxy_c - sxy_mx + (syy_py - syy_c) + z_backward(syz_c)
                force_z = sxz_c - sxz_mx + (syz_c - syz_my) + z_forward(szz_c)
                push = ext_ref[9, pl.ds(r, 1), :, :]
                active = mask_of(sub, r)
                for c, force in enumerate((force_x, force_y, force_z)):
                    old = vbuf[c, pl.ds(b, 1), ys, :]
                    vbuf[c, pl.ds(b, 1), ys, :] = keep(active, old + push * force, old)
                return carry

            lax.fori_loop(lo, hi, vel_row, 0, unroll=True)

            def strs_row(b, carry, sub=sub):
                r = b - 1
                vx_c = vbuf[0, pl.ds(b, 1), ys, :]
                vx_mx = vbuf[0, pl.ds(b - 1, 1), ys, :]
                vx_py = vbuf[0, pl.ds(b, 1), yp, :]
                vy_c = vbuf[1, pl.ds(b, 1), ys, :]
                vy_my = vbuf[1, pl.ds(b, 1), ym, :]
                vy_px = vbuf[1, pl.ds(b + 1, 1), ys, :]
                vz_c = vbuf[2, pl.ds(b, 1), ys, :]
                vz_px = vbuf[2, pl.ds(b + 1, 1), ys, :]
                vz_py = vbuf[2, pl.ds(b, 1), yp, :]
                strain_x = vx_c - vx_mx
                strain_y = vy_c - vy_my
                strain_z = z_backward(vz_c)
                shear_xy = vx_py - vx_c + (vy_px - vy_c)
                shear_xz = z_forward(vx_c) + (vz_px - vz_c)
                shear_yz = z_forward(vy_c) + (vz_py - vz_c)
                trace_sum = strain_x + strain_y + strain_z
                lam = ext_ref[10, pl.ds(r, 1), :, :]
                shear = ext_ref[11, pl.ds(r, 1), :, :]
                two_shear = 2.0 * shear
                adds = (
                    lam * trace_sum + two_shear * strain_x,
                    lam * trace_sum + two_shear * strain_y,
                    shear * shear_xy,
                    shear * shear_xz,
                    shear * shear_yz,
                    lam * trace_sum + two_shear * strain_z,
                )
                active = mask_of(sub, r)
                for c, add in enumerate(adds):
                    old = sbuf[c, pl.ds(b, 1), ys, :]
                    sbuf[c, pl.ds(b, 1), ys, :] = keep(active, old + add, old)
                return carry

            lax.fori_loop(lo, hi, strs_row, 0, unroll=True)

    xs = slice(halo + 1, halo + 1 + nx)
    yc = slice(YOFF + halo, YOFF + halo + ny)
    for c in range(3):
        vel_out[c] = vbuf[c, xs, yc, :]
    for c in range(6):
        strs_out[c] = sbuf[c, xs, yc, :]


def substeps(below, mid, above, nx, ny):
    fields, piece, cols, depth = mid.shape
    rows = 3 * piece
    return pl.pallas_call(
        substeps_kernel,
        out_shape=(
            jax.ShapeDtypeStruct((3, nx, ny, depth), jnp.float32),
            jax.ShapeDtypeStruct((6, nx, ny, depth), jnp.float32),
        ),
        scratch_shapes=[
            pltpu.VMEM((3, rows + 2, cols + 2 * YOFF, depth), jnp.float32),
            pltpu.VMEM((6, rows + 2, cols + 2 * YOFF, depth), jnp.float32),
            pltpu.VMEM((fields, rows, cols, depth), jnp.float32),
        ],
        interpret=INTERPRET,
    )(below, mid, above)


def per_device(velocity, stress, buoyancy, lame_lambda, lame_mu, rate_exponent):
    nx, ny = velocity.shape[1], velocity.shape[2]
    exponent = rate_exponent[0, 0]
    scale = level_scale(exponent)
    level = jnp.full(buoyancy.shape, exponent.astype(jnp.float32))
    block = jnp.concatenate(
        [
            velocity,
            stress,
            (buoyancy * scale)[None],
            (lame_lambda * scale)[None],
            (lame_mu * scale)[None],
            level[None],
        ],
        axis=0,
    )
    block = with_blocks(block, "gy", 2)
    count = lax.axis_size("gx")
    below = lax.ppermute(block, "gx", [(i, i + 1) for i in range(count - 1)])
    above = lax.ppermute(block, "gx", [(i + 1, i) for i in range(count - 1)])
    return substeps(below, block, above, nx, ny)


def solution(mesh):
    in_specs = (
        P(None, "gx", "gy", None),
        P(None, "gx", "gy", None),
        P("gx", "gy", None),
        P("gx", "gy", None),
        P("gx", "gy", None),
        P("gx", "gy"),
    )
    out_specs = (P(None, "gx", "gy", None), P(None, "gx", "gy", None))
    return jax.shard_map(
        per_device, mesh=mesh, in_specs=in_specs, out_specs=out_specs, check_vma=False
    )
```

```python
import jax
import jax.numpy as jnp
from jax import lax
from jax.sharding import PartitionSpec as P
from jax.experimental import pallas as pl
from jax.experimental.pallas import tpu as pltpu

TILE = 8
COARSE = 2
SUBSTEPS = 4


def level_scale(exponent):
    return jnp.where(exponent == 2, 0.25, jnp.where(exponent == 1, 0.5, 1.0)).astype(jnp.float32)


def centre(field):
    return field[1:-1, 1:-1]


def plus_x(field):
    return field[2:, 1:-1]


def minus_x(field):
    return field[:-2, 1:-1]


def plus_y(field):
    return field[1:-1, 2:]


def minus_y(field):
    return field[1:-1, :-2]


def z_forward(field):
    return jnp.concatenate([field[..., 1:], jnp.zeros_like(field[..., :1])], axis=-1) - field


def z_backward(field):
    return field - jnp.concatenate([jnp.zeros_like(field[..., :1]), field[..., :-1]], axis=-1)


def velocity_forces(padded, stress_zz):
    stress_xx, stress_yy, stress_xy, stress_xz, stress_yz = (
        padded[0],
        padded[1],
        padded[2],
        padded[3],
        padded[4],
    )
    force_x = (
        plus_x(stress_xx)
        - centre(stress_xx)
        + (centre(stress_xy) - minus_y(stress_xy))
        + z_backward(centre(stress_xz))
    )
    force_y = (
        centre(stress_xy)
        - minus_x(stress_xy)
        + (plus_y(stress_yy) - centre(stress_yy))
        + z_backward(centre(stress_yz))
    )
    force_z = (
        centre(stress_xz)
        - minus_x(stress_xz)
        + (centre(stress_yz) - minus_y(stress_yz))
        + z_forward(stress_zz)
    )
    return jnp.stack([force_x, force_y, force_z])


def advance_velocity(velocity, forces, push_coef, active):
    fresh = velocity + push_coef * forces
    if active is None:
        return fresh
    return jnp.where(active, fresh, velocity)


def advance_stress(stress, vel_padded, lam_coef, shear_coef, active):
    vel_x, vel_y, vel_z = (vel_padded[0], vel_padded[1], vel_padded[2])
    strain_x = centre(vel_x) - minus_x(vel_x)
    strain_y = centre(vel_y) - minus_y(vel_y)
    strain_z = z_backward(centre(vel_z))
    shear_xy = plus_y(vel_x) - centre(vel_x) + (plus_x(vel_y) - centre(vel_y))
    shear_xz = z_forward(centre(vel_x)) + (plus_x(vel_z) - centre(vel_z))
    shear_yz = z_forward(centre(vel_y)) + (plus_y(vel_z) - centre(vel_z))
    trace_sum = strain_x + strain_y + strain_z
    two_shear = 2.0 * shear_coef
    fresh = jnp.stack(
        [
            stress[0] + (lam_coef * trace_sum + two_shear * strain_x),
            stress[1] + (lam_coef * trace_sum + two_shear * strain_y),
            stress[2] + shear_coef * shear_xy,
            stress[3] + shear_coef * shear_xz,
            stress[4] + shear_coef * shear_yz,
            stress[5] + (lam_coef * trace_sum + two_shear * strain_z),
        ]
    )
    if active is None:
        return fresh
    return jnp.where(active, fresh, stress)


def with_blocks(cells, axis, dim):
    count = lax.axis_size(axis)
    from_below = lax.ppermute(cells, axis, [(i, i + 1) for i in range(count - 1)])
    from_above = lax.ppermute(cells, axis, [(i + 1, i) for i in range(count - 1)])
    return jnp.concatenate([from_below, cells, from_above], axis=dim)


INTERPRET = False
YOFF = 8


def lane_shifts(shape):
    lane = lax.broadcasted_iota(jnp.int32, shape, len(shape) - 1)
    width = shape[-1]
    from_below = pltpu.roll(lane, 1, len(shape) - 1) == (lane + (width - 1)) % width
    first = lane == 0
    last = lane == width - 1
    axis = len(shape) - 1

    def z_backward(f):
        one, back = pltpu.roll(f, 1, axis), pltpu.roll(f, width - 1, axis)
        prev = jnp.where(first, 0.0, jnp.where(from_below, one, back))
        return f - prev

    def z_forward(f):
        one, back = pltpu.roll(f, 1, axis), pltpu.roll(f, width - 1, axis)
        nxt = jnp.where(last, 0.0, jnp.where(from_below, back, one))
        return nxt - f

    return z_backward, z_forward


def substeps_kernel(*refs):
    pieces = refs[:9]
    vel_out, strs_out, vbuf, sbuf, ext_ref = refs[9:]
    piece, side = pieces[0].shape[1], pieces[0].shape[2]
    rows, cols, depth = 3 * piece, 3 * side, pieces[0].shape[3]
    ny = vel_out.shape[2]
    nx = vel_out.shape[1]
    halo = (rows - nx) // 2
    pad_rows = vbuf.shape[2] - cols - YOFF
    zero_y = jnp.zeros((vbuf.shape[1], YOFF, depth), jnp.float32)
    zero_y2 = jnp.zeros((vbuf.shape[1], pad_rows, depth), jnp.float32)
    zero_x = jnp.zeros((1, vbuf.shape[2], depth), jnp.float32)
    for buf, count in ((vbuf, 3), (sbuf, 6)):
        for c in range(count):
            buf[c, :, 0:YOFF, :] = zero_y
            buf[c, :, YOFF + cols :, :] = zero_y2
            buf[c, 0:1, :, :] = zero_x
            buf[c, rows + 1 : rows + 2, :, :] = zero_x
    for k, src in enumerate(pieces):
        at = 1 + (k // 3) * piece
        yat = (k % 3) * side
        for c in range(3):
            vbuf[c, at : at + piece, YOFF + yat : YOFF + yat + side, :] = src[c]
        for c in range(6):
            sbuf[c, at : at + piece, YOFF + yat : YOFF + yat + side, :] = src[3 + c]
        for c in range(4):
            ext_ref[9 + c, at - 1 : at - 1 + piece, yat : yat + side, :] = src[9 + c]
    z_backward, z_forward = lane_shifts((1, cols, depth))
    ys = pl.ds(YOFF, cols)
    ym = pl.ds(YOFF - 1, cols)
    yp = pl.ds(YOFF + 1, cols)

    def mask_of(sub, r):
        if sub == 3:
            return None
        lvl = ext_ref[12, pl.ds(r, 1), :, :]
        return lvl >= 1.0 if sub == 1 else lvl == 2.0

    def keep(active, fresh, old):
        return fresh if active is None else jnp.where(active, fresh, old)

    for step in range(COARSE):
        for sub in range(SUBSTEPS):
            t = step * SUBSTEPS + sub
            lo, hi = t + 1, rows + 1 - t

            def vel_row(b, carry, sub=sub):
                r = b - 1
                sxx_c = sbuf[0, pl.ds(b, 1), ys, :]
                sxx_px = sbuf[0, pl.ds(b + 1, 1), ys, :]
                syy_c = sbuf[1, pl.ds(b, 1), ys, :]
                syy_py = sbuf[1, pl.ds(b, 1), yp, :]
                sxy_c = sbuf[2, pl.ds(b, 1), ys, :]
                sxy_my = sbuf[2, pl.ds(b, 1), ym, :]
                sxy_mx = sbuf[2, pl.ds(b - 1, 1), ys, :]
                sxz_c = sbuf[3, pl.ds(b, 1), ys, :]
                sxz_mx = sbuf[3, pl.ds(b - 1, 1), ys, :]
                syz_c = sbuf[4, pl.ds(b, 1), ys, :]
                syz_my = sbuf[4, pl.ds(b, 1), ym, :]
                szz_c = sbuf[5, pl.ds(b, 1), ys, :]
                force_x = sxx_px - sxx_c + (sxy_c - sxy_my) + z_backward(sxz_c)
                force_y = sxy_c - sxy_mx + (syy_py - syy_c) + z_backward(syz_c)
                force_z = sxz_c - sxz_mx + (syz_c - syz_my) + z_forward(szz_c)
                push = ext_ref[9, pl.ds(r, 1), :, :]
                active = mask_of(sub, r)
                for c, force in enumerate((force_x, force_y, force_z)):
                    old = vbuf[c, pl.ds(b, 1), ys, :]
                    vbuf[c, pl.ds(b, 1), ys, :] = keep(active, old + push * force, old)
                return carry

            lax.fori_loop(lo, hi, vel_row, 0, unroll=True)

            def strs_row(b, carry, sub=sub):
                r = b - 1
                vx_c = vbuf[0, pl.ds(b, 1), ys, :]
                vx_mx = vbuf[0, pl.ds(b - 1, 1), ys, :]
                vx_py = vbuf[0, pl.ds(b, 1), yp, :]
                vy_c = vbuf[1, pl.ds(b, 1), ys, :]
                vy_my = vbuf[1, pl.ds(b, 1), ym, :]
                vy_px = vbuf[1, pl.ds(b + 1, 1), ys, :]
                vz_c = vbuf[2, pl.ds(b, 1), ys, :]
                vz_px = vbuf[2, pl.ds(b + 1, 1), ys, :]
                vz_py = vbuf[2, pl.ds(b, 1), yp, :]
                strain_x = vx_c - vx_mx
                strain_y = vy_c - vy_my
                strain_z = z_backward(vz_c)
                shear_xy = vx_py - vx_c + (vy_px - vy_c)
                shear_xz = z_forward(vx_c) + (vz_px - vz_c)
                shear_yz = z_forward(vy_c) + (vz_py - vz_c)
                trace_sum = strain_x + strain_y + strain_z
                lam = ext_ref[10, pl.ds(r, 1), :, :]
                shear = ext_ref[11, pl.ds(r, 1), :, :]
                two_shear = 2.0 * shear
                adds = (
                    lam * trace_sum + two_shear * strain_x,
                    lam * trace_sum + two_shear * strain_y,
                    shear * shear_xy,
                    shear * shear_xz,
                    shear * shear_yz,
                    lam * trace_sum + two_shear * strain_z,
                )
                active = mask_of(sub, r)
                for c, add in enumerate(adds):
                    old = sbuf[c, pl.ds(b, 1), ys, :]
                    sbuf[c, pl.ds(b, 1), ys, :] = keep(active, old + add, old)
                return carry

            lax.fori_loop(lo, hi, strs_row, 0, unroll=True)

    xs = slice(halo + 1, halo + 1 + nx)
    yc = slice(YOFF + halo, YOFF + halo + ny)
    for c in range(3):
        vel_out[c] = vbuf[c, xs, yc, :]
    for c in range(6):
        strs_out[c] = sbuf[c, xs, yc, :]


def substeps(pieces, nx, ny):
    fields, piece, side, depth = pieces[0].shape
    rows, cols = 3 * piece, 3 * side
    return pl.pallas_call(
        substeps_kernel,
        out_shape=(
            jax.ShapeDtypeStruct((3, nx, ny, depth), jnp.float32),
            jax.ShapeDtypeStruct((6, nx, ny, depth), jnp.float32),
        ),
        scratch_shapes=[
            pltpu.VMEM((3, rows + 2, cols + 2 * YOFF, depth), jnp.float32),
            pltpu.VMEM((6, rows + 2, cols + 2 * YOFF, depth), jnp.float32),
            pltpu.VMEM((fields, rows, cols, depth), jnp.float32),
        ],
        interpret=INTERPRET,
    )(*pieces)


def neighbour_blocks(block):
    count_x, count_y = lax.axis_size("gx"), lax.axis_size("gy")
    pieces = []
    for i in (-1, 0, 1):
        for j in (-1, 0, 1):
            if i == 0 and j == 0:
                pieces.append(block)
            elif i == 0:
                pairs = [(b + j, b) for b in range(count_y) if 0 <= b + j < count_y]
                pieces.append(lax.ppermute(block, "gy", pairs))
            elif j == 0:
                pairs = [(a + i, a) for a in range(count_x) if 0 <= a + i < count_x]
                pieces.append(lax.ppermute(block, "gx", pairs))
            else:
                pairs = [
                    ((a + i) * count_y + b + j, a * count_y + b)
                    for a in range(count_x)
                    for b in range(count_y)
                    if 0 <= a + i < count_x and 0 <= b + j < count_y
                ]
                pieces.append(lax.ppermute(block, ("gx", "gy"), pairs))
    return pieces


def per_device(velocity, stress, buoyancy, lame_lambda, lame_mu, rate_exponent):
    nx, ny = velocity.shape[1], velocity.shape[2]
    exponent = rate_exponent[0, 0]
    scale = level_scale(exponent)
    level = jnp.full(buoyancy.shape, exponent.astype(jnp.float32))
    block = jnp.concatenate(
        [
            velocity,
            stress,
            (buoyancy * scale)[None],
            (lame_lambda * scale)[None],
            (lame_mu * scale)[None],
            level[None],
        ],
        axis=0,
    )
    return substeps(neighbour_blocks(block), nx, ny)


def solution(mesh):
    in_specs = (
        P(None, "gx", "gy", None),
        P(None, "gx", "gy", None),
        P("gx", "gy", None),
        P("gx", "gy", None),
        P("gx", "gy", None),
        P("gx", "gy"),
    )
    out_specs = (P(None, "gx", "gy", None), P(None, "gx", "gy", None))
    return jax.shard_map(
        per_device, mesh=mesh, in_specs=in_specs, out_specs=out_specs, check_vma=False
    )
```

```python
import jax
import jax.numpy as jnp
from jax import lax
from jax.sharding import PartitionSpec as P
from jax.experimental import pallas as pl
from jax.experimental.pallas import tpu as pltpu

TILE = 8
COARSE = 2
SUBSTEPS = 4


def level_scale(exponent):
    return jnp.where(exponent == 2, 0.25, jnp.where(exponent == 1, 0.5, 1.0)).astype(jnp.float32)


def centre(field):
    return field[1:-1, 1:-1]


def plus_x(field):
    return field[2:, 1:-1]


def minus_x(field):
    return field[:-2, 1:-1]


def plus_y(field):
    return field[1:-1, 2:]


def minus_y(field):
    return field[1:-1, :-2]


def z_forward(field):
    return jnp.concatenate([field[..., 1:], jnp.zeros_like(field[..., :1])], axis=-1) - field


def z_backward(field):
    return field - jnp.concatenate([jnp.zeros_like(field[..., :1]), field[..., :-1]], axis=-1)


def velocity_forces(padded, stress_zz):
    stress_xx, stress_yy, stress_xy, stress_xz, stress_yz = (
        padded[0],
        padded[1],
        padded[2],
        padded[3],
        padded[4],
    )
    force_x = (
        plus_x(stress_xx)
        - centre(stress_xx)
        + (centre(stress_xy) - minus_y(stress_xy))
        + z_backward(centre(stress_xz))
    )
    force_y = (
        centre(stress_xy)
        - minus_x(stress_xy)
        + (plus_y(stress_yy) - centre(stress_yy))
        + z_backward(centre(stress_yz))
    )
    force_z = (
        centre(stress_xz)
        - minus_x(stress_xz)
        + (centre(stress_yz) - minus_y(stress_yz))
        + z_forward(stress_zz)
    )
    return jnp.stack([force_x, force_y, force_z])


def advance_velocity(velocity, forces, push_coef, active):
    fresh = velocity + push_coef * forces
    if active is None:
        return fresh
    return jnp.where(active, fresh, velocity)


def advance_stress(stress, vel_padded, lam_coef, shear_coef, active):
    vel_x, vel_y, vel_z = (vel_padded[0], vel_padded[1], vel_padded[2])
    strain_x = centre(vel_x) - minus_x(vel_x)
    strain_y = centre(vel_y) - minus_y(vel_y)
    strain_z = z_backward(centre(vel_z))
    shear_xy = plus_y(vel_x) - centre(vel_x) + (plus_x(vel_y) - centre(vel_y))
    shear_xz = z_forward(centre(vel_x)) + (plus_x(vel_z) - centre(vel_z))
    shear_yz = z_forward(centre(vel_y)) + (plus_y(vel_z) - centre(vel_z))
    trace_sum = strain_x + strain_y + strain_z
    two_shear = 2.0 * shear_coef
    fresh = jnp.stack(
        [
            stress[0] + (lam_coef * trace_sum + two_shear * strain_x),
            stress[1] + (lam_coef * trace_sum + two_shear * strain_y),
            stress[2] + shear_coef * shear_xy,
            stress[3] + shear_coef * shear_xz,
            stress[4] + shear_coef * shear_yz,
            stress[5] + (lam_coef * trace_sum + two_shear * strain_z),
        ]
    )
    if active is None:
        return fresh
    return jnp.where(active, fresh, stress)


def with_blocks(cells, axis, dim):
    count = lax.axis_size(axis)
    from_below = lax.ppermute(cells, axis, [(i, i + 1) for i in range(count - 1)])
    from_above = lax.ppermute(cells, axis, [(i + 1, i) for i in range(count - 1)])
    return jnp.concatenate([from_below, cells, from_above], axis=dim)


INTERPRET = False
YOFF = 8


def lane_shifts(shape):
    lane = lax.broadcasted_iota(jnp.int32, shape, len(shape) - 1)
    width = shape[-1]
    from_below = pltpu.roll(lane, 1, len(shape) - 1) == (lane + (width - 1)) % width
    first = lane == 0
    last = lane == width - 1
    axis = len(shape) - 1

    def z_backward(f):
        one, back = pltpu.roll(f, 1, axis), pltpu.roll(f, width - 1, axis)
        prev = jnp.where(first, 0.0, jnp.where(from_below, one, back))
        return f - prev

    def z_forward(f):
        one, back = pltpu.roll(f, 1, axis), pltpu.roll(f, width - 1, axis)
        nxt = jnp.where(last, 0.0, jnp.where(from_below, back, one))
        return nxt - f

    return z_backward, z_forward


def substeps_kernel(below_ref, mid_ref, above_ref, vel_out, strs_out, vbuf, sbuf, ext_ref):
    piece = mid_ref.shape[1]
    rows, cols, depth = 3 * piece, mid_ref.shape[2], mid_ref.shape[3]
    ny = vel_out.shape[2]
    nx = vel_out.shape[1]
    halo = (rows - nx) // 2
    pad_rows = vbuf.shape[2] - cols - YOFF
    zero_y = jnp.zeros((vbuf.shape[1], YOFF, depth), jnp.float32)
    zero_y2 = jnp.zeros((vbuf.shape[1], pad_rows, depth), jnp.float32)
    zero_x = jnp.zeros((1, vbuf.shape[2], depth), jnp.float32)
    for buf, count in ((vbuf, 3), (sbuf, 6)):
        for c in range(count):
            buf[c, :, 0:YOFF, :] = zero_y
            buf[c, :, YOFF + cols :, :] = zero_y2
            buf[c, 0:1, :, :] = zero_x
            buf[c, rows + 1 : rows + 2, :, :] = zero_x
    for k, src in enumerate((below_ref, mid_ref, above_ref)):
        at = 1 + k * piece
        for c in range(3):
            vbuf[c, at : at + piece, YOFF : YOFF + cols, :] = src[c]
        for c in range(6):
            sbuf[c, at : at + piece, YOFF : YOFF + cols, :] = src[3 + c]
        for c in range(3):
            ext_ref[9 + c, at - 1 : at - 1 + piece, :, :] = src[9 + c]
    z_backward, z_forward = lane_shifts((1, cols, depth))
    ys = pl.ds(YOFF, cols)
    ym = pl.ds(YOFF - 1, cols)
    yp = pl.ds(YOFF + 1, cols)

    def mask_of(sub, r):
        if sub == 3:
            return None
        field = 10 if sub == 1 else 11
        return ext_ref[field, pl.ds(r, 1), :, :] < 0.0

    def keep(active, fresh, old):
        return fresh if active is None else jnp.where(active, fresh, old)

    for step in range(COARSE):
        for sub in range(SUBSTEPS):
            t = step * SUBSTEPS + sub
            lo, hi = t + 1, rows + 1 - t

            def vel_row(b, carry, sub=sub):
                r = b - 1
                sxx_c = sbuf[0, pl.ds(b, 1), ys, :]
                sxx_px = sbuf[0, pl.ds(b + 1, 1), ys, :]
                syy_c = sbuf[1, pl.ds(b, 1), ys, :]
                syy_py = sbuf[1, pl.ds(b, 1), yp, :]
                sxy_c = sbuf[2, pl.ds(b, 1), ys, :]
                sxy_my = sbuf[2, pl.ds(b, 1), ym, :]
                sxy_mx = sbuf[2, pl.ds(b - 1, 1), ys, :]
                sxz_c = sbuf[3, pl.ds(b, 1), ys, :]
                sxz_mx = sbuf[3, pl.ds(b - 1, 1), ys, :]
                syz_c = sbuf[4, pl.ds(b, 1), ys, :]
                syz_my = sbuf[4, pl.ds(b, 1), ym, :]
                szz_c = sbuf[5, pl.ds(b, 1), ys, :]
                force_x = sxx_px - sxx_c + (sxy_c - sxy_my) + z_backward(sxz_c)
                force_y = sxy_c - sxy_mx + (syy_py - syy_c) + z_backward(syz_c)
                force_z = sxz_c - sxz_mx + (syz_c - syz_my) + z_forward(szz_c)
                push = ext_ref[9, pl.ds(r, 1), :, :]
                active = mask_of(sub, r)
                for c, force in enumerate((force_x, force_y, force_z)):
                    old = vbuf[c, pl.ds(b, 1), ys, :]
                    vbuf[c, pl.ds(b, 1), ys, :] = keep(active, old + push * force, old)
                return carry

            lax.fori_loop(lo, hi, vel_row, 0, unroll=True)

            def strs_row(b, carry, sub=sub):
                r = b - 1
                vx_c = vbuf[0, pl.ds(b, 1), ys, :]
                vx_mx = vbuf[0, pl.ds(b - 1, 1), ys, :]
                vx_py = vbuf[0, pl.ds(b, 1), yp, :]
                vy_c = vbuf[1, pl.ds(b, 1), ys, :]
                vy_my = vbuf[1, pl.ds(b, 1), ym, :]
                vy_px = vbuf[1, pl.ds(b + 1, 1), ys, :]
                vz_c = vbuf[2, pl.ds(b, 1), ys, :]
                vz_px = vbuf[2, pl.ds(b + 1, 1), ys, :]
                vz_py = vbuf[2, pl.ds(b, 1), yp, :]
                strain_x = vx_c - vx_mx
                strain_y = vy_c - vy_my
                strain_z = z_backward(vz_c)
                shear_xy = vx_py - vx_c + (vy_px - vy_c)
                shear_xz = z_forward(vx_c) + (vz_px - vz_c)
                shear_yz = z_forward(vy_c) + (vz_py - vz_c)
                trace_sum = strain_x + strain_y + strain_z
                lam = jnp.abs(ext_ref[10, pl.ds(r, 1), :, :])
                shear = jnp.abs(ext_ref[11, pl.ds(r, 1), :, :])
                two_shear = 2.0 * shear
                adds = (
                    lam * trace_sum + two_shear * strain_x,
                    lam * trace_sum + two_shear * strain_y,
                    shear * shear_xy,
                    shear * shear_xz,
                    shear * shear_yz,
                    lam * trace_sum + two_shear * strain_z,
                )
                active = mask_of(sub, r)
                for c, add in enumerate(adds):
                    old = sbuf[c, pl.ds(b, 1), ys, :]
                    sbuf[c, pl.ds(b, 1), ys, :] = keep(active, old + add, old)
                return carry

            lax.fori_loop(lo, hi, strs_row, 0, unroll=True)

    xs = slice(halo + 1, halo + 1 + nx)
    yc = slice(YOFF + halo, YOFF + halo + ny)
    for c in range(3):
        vel_out[c] = vbuf[c, xs, yc, :]
    for c in range(6):
        strs_out[c] = sbuf[c, xs, yc, :]


def substeps(below, mid, above, nx, ny):
    fields, piece, cols, depth = mid.shape
    rows = 3 * piece
    return pl.pallas_call(
        substeps_kernel,
        out_shape=(
            jax.ShapeDtypeStruct((3, nx, ny, depth), jnp.float32),
            jax.ShapeDtypeStruct((6, nx, ny, depth), jnp.float32),
        ),
        scratch_shapes=[
            pltpu.VMEM((3, rows + 2, cols + 2 * YOFF, depth), jnp.float32),
            pltpu.VMEM((6, rows + 2, cols + 2 * YOFF, depth), jnp.float32),
            pltpu.VMEM((fields, rows, cols, depth), jnp.float32),
        ],
        interpret=INTERPRET,
    )(below, mid, above)


def pack_kernel(e_ref, v_ref, s_ref, b_ref, l_ref, m_ref, out_ref):
    e = e_ref[0, 0]
    scale = jnp.where(e == 2, 0.25, jnp.where(e == 1, 0.5, 1.0)).astype(jnp.float32)
    lam_sign = jnp.where(e >= 1, -1.0, 1.0).astype(jnp.float32)
    shear_sign = jnp.where(e == 2, -1.0, 1.0).astype(jnp.float32)
    for c in range(3):
        out_ref[c] = v_ref[c]
    for c in range(6):
        out_ref[3 + c] = s_ref[c]
    out_ref[9] = b_ref[...] * scale
    out_ref[10] = (l_ref[...] * scale) * lam_sign
    out_ref[11] = (m_ref[...] * scale) * shear_sign


def pack(velocity, stress, buoyancy, lame_lambda, lame_mu, rate_exponent):
    nx, ny, depth = buoyancy.shape
    vmem = pl.BlockSpec(memory_space=pltpu.VMEM)
    return pl.pallas_call(
        pack_kernel,
        out_shape=jax.ShapeDtypeStruct((12, nx, ny, depth), jnp.float32),
        in_specs=[pl.BlockSpec(memory_space=pltpu.SMEM)] + [vmem] * 5,
        out_specs=vmem,
        interpret=INTERPRET,
    )(rate_exponent, velocity, stress, buoyancy, lame_lambda, lame_mu)


def per_device(velocity, stress, buoyancy, lame_lambda, lame_mu, rate_exponent):
    nx, ny = velocity.shape[1], velocity.shape[2]
    block = pack(velocity, stress, buoyancy, lame_lambda, lame_mu, rate_exponent)
    block = with_blocks(block, "gy", 2)
    count = lax.axis_size("gx")
    below = lax.ppermute(block, "gx", [(i, i + 1) for i in range(count - 1)])
    above = lax.ppermute(block, "gx", [(i + 1, i) for i in range(count - 1)])
    return substeps(below, block, above, nx, ny)


def solution(mesh):
    in_specs = (
        P(None, "gx", "gy", None),
        P(None, "gx", "gy", None),
        P("gx", "gy", None),
        P("gx", "gy", None),
        P("gx", "gy", None),
        P("gx", "gy"),
    )
    out_specs = (P(None, "gx", "gy", None), P(None, "gx", "gy", None))
    return jax.shard_map(
        per_device, mesh=mesh, in_specs=in_specs, out_specs=out_specs, check_vma=False
    )
```

```python
import jax
import jax.numpy as jnp
from jax import lax
from jax.sharding import PartitionSpec as P
from jax.experimental import pallas as pl
from jax.experimental.pallas import tpu as pltpu

TILE = 8
COARSE = 2
SUBSTEPS = 4


def level_scale(exponent):
    return jnp.where(exponent == 2, 0.25, jnp.where(exponent == 1, 0.5, 1.0)).astype(jnp.float32)


def centre(field):
    return field[1:-1, 1:-1]


def plus_x(field):
    return field[2:, 1:-1]


def minus_x(field):
    return field[:-2, 1:-1]


def plus_y(field):
    return field[1:-1, 2:]


def minus_y(field):
    return field[1:-1, :-2]


def z_forward(field):
    return jnp.concatenate([field[..., 1:], jnp.zeros_like(field[..., :1])], axis=-1) - field


def z_backward(field):
    return field - jnp.concatenate([jnp.zeros_like(field[..., :1]), field[..., :-1]], axis=-1)


def velocity_forces(padded, stress_zz):
    stress_xx, stress_yy, stress_xy, stress_xz, stress_yz = (
        padded[0],
        padded[1],
        padded[2],
        padded[3],
        padded[4],
    )
    force_x = (
        plus_x(stress_xx)
        - centre(stress_xx)
        + (centre(stress_xy) - minus_y(stress_xy))
        + z_backward(centre(stress_xz))
    )
    force_y = (
        centre(stress_xy)
        - minus_x(stress_xy)
        + (plus_y(stress_yy) - centre(stress_yy))
        + z_backward(centre(stress_yz))
    )
    force_z = (
        centre(stress_xz)
        - minus_x(stress_xz)
        + (centre(stress_yz) - minus_y(stress_yz))
        + z_forward(stress_zz)
    )
    return jnp.stack([force_x, force_y, force_z])


def advance_velocity(velocity, forces, push_coef, active):
    fresh = velocity + push_coef * forces
    if active is None:
        return fresh
    return jnp.where(active, fresh, velocity)


def advance_stress(stress, vel_padded, lam_coef, shear_coef, active):
    vel_x, vel_y, vel_z = (vel_padded[0], vel_padded[1], vel_padded[2])
    strain_x = centre(vel_x) - minus_x(vel_x)
    strain_y = centre(vel_y) - minus_y(vel_y)
    strain_z = z_backward(centre(vel_z))
    shear_xy = plus_y(vel_x) - centre(vel_x) + (plus_x(vel_y) - centre(vel_y))
    shear_xz = z_forward(centre(vel_x)) + (plus_x(vel_z) - centre(vel_z))
    shear_yz = z_forward(centre(vel_y)) + (plus_y(vel_z) - centre(vel_z))
    trace_sum = strain_x + strain_y + strain_z
    two_shear = 2.0 * shear_coef
    fresh = jnp.stack(
        [
            stress[0] + (lam_coef * trace_sum + two_shear * strain_x),
            stress[1] + (lam_coef * trace_sum + two_shear * strain_y),
            stress[2] + shear_coef * shear_xy,
            stress[3] + shear_coef * shear_xz,
            stress[4] + shear_coef * shear_yz,
            stress[5] + (lam_coef * trace_sum + two_shear * strain_z),
        ]
    )
    if active is None:
        return fresh
    return jnp.where(active, fresh, stress)


def with_blocks(cells, axis, dim):
    count = lax.axis_size(axis)
    from_below = lax.ppermute(cells, axis, [(i, i + 1) for i in range(count - 1)])
    from_above = lax.ppermute(cells, axis, [(i + 1, i) for i in range(count - 1)])
    return jnp.concatenate([from_below, cells, from_above], axis=dim)


INTERPRET = False
YOFF = 8


def lane_shifts(shape):
    lane = lax.broadcasted_iota(jnp.int32, shape, len(shape) - 1)
    width = shape[-1]
    from_below = pltpu.roll(lane, 1, len(shape) - 1) == (lane + (width - 1)) % width
    first = lane == 0
    last = lane == width - 1
    axis = len(shape) - 1

    def z_backward(f):
        one, back = pltpu.roll(f, 1, axis), pltpu.roll(f, width - 1, axis)
        prev = jnp.where(first, 0.0, jnp.where(from_below, one, back))
        return f - prev

    def z_forward(f):
        one, back = pltpu.roll(f, 1, axis), pltpu.roll(f, width - 1, axis)
        nxt = jnp.where(last, 0.0, jnp.where(from_below, back, one))
        return nxt - f

    return z_backward, z_forward


def substeps_kernel(*refs):
    d_below, x_below, y_below, own, y_above, d_above, x_above = refs[:7]
    vel_out, strs_out, vbuf, sbuf, ext_ref = refs[7:]
    piece, side, depth = own.shape[1], own.shape[2], own.shape[3]
    rows, cols = 3 * piece, 3 * side
    ny = vel_out.shape[2]
    nx = vel_out.shape[1]
    halo = (rows - nx) // 2
    pad_rows = vbuf.shape[2] - cols - YOFF
    zero_y = jnp.zeros((vbuf.shape[1], YOFF, depth), jnp.float32)
    zero_y2 = jnp.zeros((vbuf.shape[1], pad_rows, depth), jnp.float32)
    zero_x = jnp.zeros((1, vbuf.shape[2], depth), jnp.float32)
    for buf, count in ((vbuf, 3), (sbuf, 6)):
        for c in range(count):
            buf[c, :, 0:YOFF, :] = zero_y
            buf[c, :, YOFF + cols :, :] = zero_y2
            buf[c, 0:1, :, :] = zero_x
            buf[c, rows + 1 : rows + 2, :, :] = zero_x
    placed = (
        (d_below, 0, 0, 0),
        (d_below, 0, 2, side),
        (x_below, 0, 1, 0),
        (y_below, 1, 0, 0),
        (own, 1, 1, 0),
        (y_above, 1, 2, 0),
        (d_above, 2, 0, 0),
        (d_above, 2, 2, side),
        (x_above, 2, 1, 0),
    )
    for src, xb, yb, yfrom in placed:
        at = 1 + xb * piece
        yat = yb * side
        yin = slice(yfrom, yfrom + side)
        for c in range(3):
            vbuf[c, at : at + piece, YOFF + yat : YOFF + yat + side, :] = src[c, :, yin, :]
        for c in range(6):
            sbuf[c, at : at + piece, YOFF + yat : YOFF + yat + side, :] = src[3 + c, :, yin, :]
        for c in range(3):
            ext_ref[9 + c, at - 1 : at - 1 + piece, yat : yat + side, :] = src[9 + c, :, yin, :]
    z_backward, z_forward = lane_shifts((1, cols, depth))
    ys = pl.ds(YOFF, cols)
    ym = pl.ds(YOFF - 1, cols)
    yp = pl.ds(YOFF + 1, cols)

    def mask_of(sub, r):
        if sub == 3:
            return None
        field = 10 if sub == 1 else 11
        return ext_ref[field, pl.ds(r, 1), :, :] < 0.0

    def keep(active, fresh, old):
        return fresh if active is None else jnp.where(active, fresh, old)

    for step in range(COARSE):
        for sub in range(SUBSTEPS):
            t = step * SUBSTEPS + sub
            lo, hi = t + 1, rows + 1 - t

            def vel_row(b, carry, sub=sub):
                r = b - 1
                sxx_c = sbuf[0, pl.ds(b, 1), ys, :]
                sxx_px = sbuf[0, pl.ds(b + 1, 1), ys, :]
                syy_c = sbuf[1, pl.ds(b, 1), ys, :]
                syy_py = sbuf[1, pl.ds(b, 1), yp, :]
                sxy_c = sbuf[2, pl.ds(b, 1), ys, :]
                sxy_my = sbuf[2, pl.ds(b, 1), ym, :]
                sxy_mx = sbuf[2, pl.ds(b - 1, 1), ys, :]
                sxz_c = sbuf[3, pl.ds(b, 1), ys, :]
                sxz_mx = sbuf[3, pl.ds(b - 1, 1), ys, :]
                syz_c = sbuf[4, pl.ds(b, 1), ys, :]
                syz_my = sbuf[4, pl.ds(b, 1), ym, :]
                szz_c = sbuf[5, pl.ds(b, 1), ys, :]
                force_x = sxx_px - sxx_c + (sxy_c - sxy_my) + z_backward(sxz_c)
                force_y = sxy_c - sxy_mx + (syy_py - syy_c) + z_backward(syz_c)
                force_z = sxz_c - sxz_mx + (syz_c - syz_my) + z_forward(szz_c)
                push = ext_ref[9, pl.ds(r, 1), :, :]
                active = mask_of(sub, r)
                for c, force in enumerate((force_x, force_y, force_z)):
                    old = vbuf[c, pl.ds(b, 1), ys, :]
                    vbuf[c, pl.ds(b, 1), ys, :] = keep(active, old + push * force, old)
                return carry

            lax.fori_loop(lo, hi, vel_row, 0, unroll=True)

            def strs_row(b, carry, sub=sub):
                r = b - 1
                vx_c = vbuf[0, pl.ds(b, 1), ys, :]
                vx_mx = vbuf[0, pl.ds(b - 1, 1), ys, :]
                vx_py = vbuf[0, pl.ds(b, 1), yp, :]
                vy_c = vbuf[1, pl.ds(b, 1), ys, :]
                vy_my = vbuf[1, pl.ds(b, 1), ym, :]
                vy_px = vbuf[1, pl.ds(b + 1, 1), ys, :]
                vz_c = vbuf[2, pl.ds(b, 1), ys, :]
                vz_px = vbuf[2, pl.ds(b + 1, 1), ys, :]
                vz_py = vbuf[2, pl.ds(b, 1), yp, :]
                strain_x = vx_c - vx_mx
                strain_y = vy_c - vy_my
                strain_z = z_backward(vz_c)
                shear_xy = vx_py - vx_c + (vy_px - vy_c)
                shear_xz = z_forward(vx_c) + (vz_px - vz_c)
                shear_yz = z_forward(vy_c) + (vz_py - vz_c)
                trace_sum = strain_x + strain_y + strain_z
                lam = jnp.abs(ext_ref[10, pl.ds(r, 1), :, :])
                shear = jnp.abs(ext_ref[11, pl.ds(r, 1), :, :])
                two_shear = 2.0 * shear
                adds = (
                    lam * trace_sum + two_shear * strain_x,
                    lam * trace_sum + two_shear * strain_y,
                    shear * shear_xy,
                    shear * shear_xz,
                    shear * shear_yz,
                    lam * trace_sum + two_shear * strain_z,
                )
                active = mask_of(sub, r)
                for c, add in enumerate(adds):
                    old = sbuf[c, pl.ds(b, 1), ys, :]
                    sbuf[c, pl.ds(b, 1), ys, :] = keep(active, old + add, old)
                return carry

            lax.fori_loop(lo, hi, strs_row, 0, unroll=True)

    xs = slice(halo + 1, halo + 1 + nx)
    yc = slice(YOFF + halo, YOFF + halo + ny)
    for c in range(3):
        vel_out[c] = vbuf[c, xs, yc, :]
    for c in range(6):
        strs_out[c] = sbuf[c, xs, yc, :]


def substeps(pieces, nx, ny):
    fields, piece, side, depth = pieces[3].shape
    rows, cols = 3 * piece, 3 * side
    return pl.pallas_call(
        substeps_kernel,
        out_shape=(
            jax.ShapeDtypeStruct((3, nx, ny, depth), jnp.float32),
            jax.ShapeDtypeStruct((6, nx, ny, depth), jnp.float32),
        ),
        scratch_shapes=[
            pltpu.VMEM((3, rows + 2, cols + 2 * YOFF, depth), jnp.float32),
            pltpu.VMEM((6, rows + 2, cols + 2 * YOFF, depth), jnp.float32),
            pltpu.VMEM((fields, rows, cols, depth), jnp.float32),
        ],
        interpret=INTERPRET,
    )(*pieces)


def pack_kernel(e_ref, v_ref, s_ref, b_ref, l_ref, m_ref, out_ref):
    e = e_ref[0, 0]
    scale = jnp.where(e == 2, 0.25, jnp.where(e == 1, 0.5, 1.0)).astype(jnp.float32)
    lam_sign = jnp.where(e >= 1, -1.0, 1.0).astype(jnp.float32)
    shear_sign = jnp.where(e == 2, -1.0, 1.0).astype(jnp.float32)
    for c in range(3):
        out_ref[c] = v_ref[c]
    for c in range(6):
        out_ref[3 + c] = s_ref[c]
    out_ref[9] = b_ref[...] * scale
    out_ref[10] = (l_ref[...] * scale) * lam_sign
    out_ref[11] = (m_ref[...] * scale) * shear_sign


def pack(velocity, stress, buoyancy, lame_lambda, lame_mu, rate_exponent):
    nx, ny, depth = buoyancy.shape
    vmem = pl.BlockSpec(memory_space=pltpu.VMEM)
    return pl.pallas_call(
        pack_kernel,
        out_shape=jax.ShapeDtypeStruct((12, nx, ny, depth), jnp.float32),
        in_specs=[pl.BlockSpec(memory_space=pltpu.SMEM)] + [vmem] * 5,
        out_specs=vmem,
        interpret=INTERPRET,
    )(rate_exponent, velocity, stress, buoyancy, lame_lambda, lame_mu)


def per_device(velocity, stress, buoyancy, lame_lambda, lame_mu, rate_exponent):
    nx, ny = velocity.shape[1], velocity.shape[2]
    block = pack(velocity, stress, buoyancy, lame_lambda, lame_mu, rate_exponent)
    count_x, count_y = lax.axis_size("gx"), lax.axis_size("gy")
    up_x = [(i, i + 1) for i in range(count_x - 1)]
    down_x = [(i + 1, i) for i in range(count_x - 1)]
    y_below = lax.ppermute(block, "gy", [(i, i + 1) for i in range(count_y - 1)])
    y_above = lax.ppermute(block, "gy", [(i + 1, i) for i in range(count_y - 1)])
    x_below = lax.ppermute(block, "gx", up_x)
    x_above = lax.ppermute(block, "gx", down_x)
    y_below, y_above, x_below, x_above = lax.optimization_barrier((y_below, y_above, x_below, x_above))
    y_pair = jnp.concatenate([y_below, y_above], axis=2)
    d_below = lax.ppermute(y_pair, "gx", up_x)
    d_above = lax.ppermute(y_pair, "gx", down_x)
    pieces = (d_below, x_below, y_below, block, y_above, d_above, x_above)
    return substeps(pieces, nx, ny)


def solution(mesh):
    in_specs = (
        P(None, "gx", "gy", None),
        P(None, "gx", "gy", None),
        P("gx", "gy", None),
        P("gx", "gy", None),
        P("gx", "gy", None),
        P("gx", "gy"),
    )
    out_specs = (P(None, "gx", "gy", None), P(None, "gx", "gy", None))
    return jax.shard_map(
        per_device, mesh=mesh, in_specs=in_specs, out_specs=out_specs, check_vma=False
    )
```

```python
import jax
import jax.numpy as jnp
from jax import lax
from jax.sharding import PartitionSpec as P
from jax.experimental import pallas as pl
from jax.experimental.pallas import tpu as pltpu

TILE = 8
COARSE = 2
SUBSTEPS = 4


def level_scale(exponent):
    return jnp.where(exponent == 2, 0.25, jnp.where(exponent == 1, 0.5, 1.0)).astype(jnp.float32)


def centre(field):
    return field[1:-1, 1:-1]


def plus_x(field):
    return field[2:, 1:-1]


def minus_x(field):
    return field[:-2, 1:-1]


def plus_y(field):
    return field[1:-1, 2:]


def minus_y(field):
    return field[1:-1, :-2]


def z_forward(field):
    return jnp.concatenate([field[..., 1:], jnp.zeros_like(field[..., :1])], axis=-1) - field


def z_backward(field):
    return field - jnp.concatenate([jnp.zeros_like(field[..., :1]), field[..., :-1]], axis=-1)


def velocity_forces(padded, stress_zz):
    stress_xx, stress_yy, stress_xy, stress_xz, stress_yz = (
        padded[0],
        padded[1],
        padded[2],
        padded[3],
        padded[4],
    )
    force_x = (
        plus_x(stress_xx)
        - centre(stress_xx)
        + (centre(stress_xy) - minus_y(stress_xy))
        + z_backward(centre(stress_xz))
    )
    force_y = (
        centre(stress_xy)
        - minus_x(stress_xy)
        + (plus_y(stress_yy) - centre(stress_yy))
        + z_backward(centre(stress_yz))
    )
    force_z = (
        centre(stress_xz)
        - minus_x(stress_xz)
        + (centre(stress_yz) - minus_y(stress_yz))
        + z_forward(stress_zz)
    )
    return jnp.stack([force_x, force_y, force_z])


def advance_velocity(velocity, forces, push_coef, active):
    fresh = velocity + push_coef * forces
    if active is None:
        return fresh
    return jnp.where(active, fresh, velocity)


def advance_stress(stress, vel_padded, lam_coef, shear_coef, active):
    vel_x, vel_y, vel_z = (vel_padded[0], vel_padded[1], vel_padded[2])
    strain_x = centre(vel_x) - minus_x(vel_x)
    strain_y = centre(vel_y) - minus_y(vel_y)
    strain_z = z_backward(centre(vel_z))
    shear_xy = plus_y(vel_x) - centre(vel_x) + (plus_x(vel_y) - centre(vel_y))
    shear_xz = z_forward(centre(vel_x)) + (plus_x(vel_z) - centre(vel_z))
    shear_yz = z_forward(centre(vel_y)) + (plus_y(vel_z) - centre(vel_z))
    trace_sum = strain_x + strain_y + strain_z
    two_shear = 2.0 * shear_coef
    fresh = jnp.stack(
        [
            stress[0] + (lam_coef * trace_sum + two_shear * strain_x),
            stress[1] + (lam_coef * trace_sum + two_shear * strain_y),
            stress[2] + shear_coef * shear_xy,
            stress[3] + shear_coef * shear_xz,
            stress[4] + shear_coef * shear_yz,
            stress[5] + (lam_coef * trace_sum + two_shear * strain_z),
        ]
    )
    if active is None:
        return fresh
    return jnp.where(active, fresh, stress)


def with_blocks(cells, axis, dim):
    count = lax.axis_size(axis)
    from_below = lax.ppermute(cells, axis, [(i, i + 1) for i in range(count - 1)])
    from_above = lax.ppermute(cells, axis, [(i + 1, i) for i in range(count - 1)])
    return jnp.concatenate([from_below, cells, from_above], axis=dim)


INTERPRET = False
YOFF = 8


def lane_shifts(shape):
    axis = len(shape) - 1
    width = shape[-1]
    lane = lax.broadcasted_iota(jnp.int32, shape, axis)
    first = lane == 0
    last = lane == width - 1

    def z_backward(f):
        return f - jnp.where(first, 0.0, pltpu.roll(f, 1, axis))

    def z_forward(f):
        return jnp.where(last, 0.0, pltpu.roll(f, width - 1, axis)) - f

    return z_backward, z_forward


def substeps_kernel(below_ref, mid_ref, above_ref, vel_out, strs_out, vbuf, sbuf, ext_ref):
    piece = mid_ref.shape[1]
    rows, cols, depth = 3 * piece, mid_ref.shape[2], mid_ref.shape[3]
    ny = vel_out.shape[2]
    nx = vel_out.shape[1]
    halo = (rows - nx) // 2
    pad_rows = vbuf.shape[2] - cols - YOFF
    zero_y = jnp.zeros((vbuf.shape[1], YOFF, depth), jnp.float32)
    zero_y2 = jnp.zeros((vbuf.shape[1], pad_rows, depth), jnp.float32)
    zero_x = jnp.zeros((1, vbuf.shape[2], depth), jnp.float32)
    for buf, count in ((vbuf, 3), (sbuf, 6)):
        for c in range(count):
            buf[c, :, 0:YOFF, :] = zero_y
            buf[c, :, YOFF + cols :, :] = zero_y2
            buf[c, 0:1, :, :] = zero_x
            buf[c, rows + 1 : rows + 2, :, :] = zero_x
    for k, src in enumerate((below_ref, mid_ref, above_ref)):
        at = 1 + k * piece
        for c in range(3):
            vbuf[c, at : at + piece, YOFF : YOFF + cols, :] = src[c]
        for c in range(6):
            sbuf[c, at : at + piece, YOFF : YOFF + cols, :] = src[3 + c]
        for c in range(3):
            ext_ref[9 + c, at - 1 : at - 1 + piece, :, :] = src[9 + c]
    z_backward, z_forward = lane_shifts((1, cols, depth))
    ys = pl.ds(YOFF, cols)
    ym = pl.ds(YOFF - 1, cols)
    yp = pl.ds(YOFF + 1, cols)

    def mask_of(sub, r):
        if sub == 3:
            return None
        field = 10 if sub == 1 else 11
        return ext_ref[field, pl.ds(r, 1), :, :] < 0.0

    def keep(active, fresh, old):
        return fresh if active is None else jnp.where(active, fresh, old)

    for step in range(COARSE):
        for sub in range(SUBSTEPS):
            t = step * SUBSTEPS + sub
            lo, hi = t + 1, rows + 1 - t

            def vel_row(b, carry, sub=sub):
                r = b - 1
                sxx_c = sbuf[0, pl.ds(b, 1), ys, :]
                sxx_px = sbuf[0, pl.ds(b + 1, 1), ys, :]
                syy_c = sbuf[1, pl.ds(b, 1), ys, :]
                syy_py = sbuf[1, pl.ds(b, 1), yp, :]
                sxy_c = sbuf[2, pl.ds(b, 1), ys, :]
                sxy_my = sbuf[2, pl.ds(b, 1), ym, :]
                sxy_mx = sbuf[2, pl.ds(b - 1, 1), ys, :]
                sxz_c = sbuf[3, pl.ds(b, 1), ys, :]
                sxz_mx = sbuf[3, pl.ds(b - 1, 1), ys, :]
                syz_c = sbuf[4, pl.ds(b, 1), ys, :]
                syz_my = sbuf[4, pl.ds(b, 1), ym, :]
                szz_c = sbuf[5, pl.ds(b, 1), ys, :]
                force_x = sxx_px - sxx_c + (sxy_c - sxy_my) + z_backward(sxz_c)
                force_y = sxy_c - sxy_mx + (syy_py - syy_c) + z_backward(syz_c)
                force_z = sxz_c - sxz_mx + (syz_c - syz_my) + z_forward(szz_c)
                push = ext_ref[9, pl.ds(r, 1), :, :]
                active = mask_of(sub, r)
                for c, force in enumerate((force_x, force_y, force_z)):
                    old = vbuf[c, pl.ds(b, 1), ys, :]
                    vbuf[c, pl.ds(b, 1), ys, :] = keep(active, old + push * force, old)
                return carry

            lax.fori_loop(lo, hi, vel_row, 0, unroll=True)

            def strs_row(b, carry, sub=sub):
                r = b - 1
                vx_c = vbuf[0, pl.ds(b, 1), ys, :]
                vx_mx = vbuf[0, pl.ds(b - 1, 1), ys, :]
                vx_py = vbuf[0, pl.ds(b, 1), yp, :]
                vy_c = vbuf[1, pl.ds(b, 1), ys, :]
                vy_my = vbuf[1, pl.ds(b, 1), ym, :]
                vy_px = vbuf[1, pl.ds(b + 1, 1), ys, :]
                vz_c = vbuf[2, pl.ds(b, 1), ys, :]
                vz_px = vbuf[2, pl.ds(b + 1, 1), ys, :]
                vz_py = vbuf[2, pl.ds(b, 1), yp, :]
                strain_x = vx_c - vx_mx
                strain_y = vy_c - vy_my
                strain_z = z_backward(vz_c)
                shear_xy = vx_py - vx_c + (vy_px - vy_c)
                shear_xz = z_forward(vx_c) + (vz_px - vz_c)
                shear_yz = z_forward(vy_c) + (vz_py - vz_c)
                trace_sum = strain_x + strain_y + strain_z
                lam = jnp.abs(ext_ref[10, pl.ds(r, 1), :, :])
                shear = jnp.abs(ext_ref[11, pl.ds(r, 1), :, :])
                two_shear = 2.0 * shear
                adds = (
                    lam * trace_sum + two_shear * strain_x,
                    lam * trace_sum + two_shear * strain_y,
                    shear * shear_xy,
                    shear * shear_xz,
                    shear * shear_yz,
                    lam * trace_sum + two_shear * strain_z,
                )
                active = mask_of(sub, r)
                for c, add in enumerate(adds):
                    old = sbuf[c, pl.ds(b, 1), ys, :]
                    sbuf[c, pl.ds(b, 1), ys, :] = keep(active, old + add, old)
                return carry

            lax.fori_loop(lo, hi, strs_row, 0, unroll=True)

    xs = slice(halo + 1, halo + 1 + nx)
    yc = slice(YOFF + halo, YOFF + halo + ny)
    for c in range(3):
        vel_out[c] = vbuf[c, xs, yc, :]
    for c in range(6):
        strs_out[c] = sbuf[c, xs, yc, :]


def substeps(below, mid, above, nx, ny):
    fields, piece, cols, depth = mid.shape
    rows = 3 * piece
    return pl.pallas_call(
        substeps_kernel,
        out_shape=(
            jax.ShapeDtypeStruct((3, nx, ny, depth), jnp.float32),
            jax.ShapeDtypeStruct((6, nx, ny, depth), jnp.float32),
        ),
        scratch_shapes=[
            pltpu.VMEM((3, rows + 2, cols + 2 * YOFF, depth), jnp.float32),
            pltpu.VMEM((6, rows + 2, cols + 2 * YOFF, depth), jnp.float32),
            pltpu.VMEM((fields, rows, cols, depth), jnp.float32),
        ],
        interpret=INTERPRET,
    )(below, mid, above)


def pack_kernel(e_ref, v_ref, s_ref, b_ref, l_ref, m_ref, out_ref):
    e = e_ref[0, 0]
    scale = jnp.where(e == 2, 0.25, jnp.where(e == 1, 0.5, 1.0)).astype(jnp.float32)
    lam_sign = jnp.where(e >= 1, -1.0, 1.0).astype(jnp.float32)
    shear_sign = jnp.where(e == 2, -1.0, 1.0).astype(jnp.float32)
    for c in range(3):
        out_ref[c] = v_ref[c]
    for c in range(6):
        out_ref[3 + c] = s_ref[c]
    out_ref[9] = b_ref[...] * scale
    out_ref[10] = (l_ref[...] * scale) * lam_sign
    out_ref[11] = (m_ref[...] * scale) * shear_sign


def pack(velocity, stress, buoyancy, lame_lambda, lame_mu, rate_exponent):
    nx, ny, depth = buoyancy.shape
    vmem = pl.BlockSpec(memory_space=pltpu.VMEM)
    return pl.pallas_call(
        pack_kernel,
        out_shape=jax.ShapeDtypeStruct((12, nx, ny, depth), jnp.float32),
        in_specs=[pl.BlockSpec(memory_space=pltpu.SMEM)] + [vmem] * 5,
        out_specs=vmem,
        interpret=INTERPRET,
    )(rate_exponent, velocity, stress, buoyancy, lame_lambda, lame_mu)


def per_device(velocity, stress, buoyancy, lame_lambda, lame_mu, rate_exponent):
    nx, ny = velocity.shape[1], velocity.shape[2]
    block = pack(velocity, stress, buoyancy, lame_lambda, lame_mu, rate_exponent)
    block = with_blocks(block, "gy", 2)
    count = lax.axis_size("gx")
    below = lax.ppermute(block, "gx", [(i, i + 1) for i in range(count - 1)])
    above = lax.ppermute(block, "gx", [(i + 1, i) for i in range(count - 1)])
    return substeps(below, block, above, nx, ny)


def solution(mesh):
    in_specs = (
        P(None, "gx", "gy", None),
        P(None, "gx", "gy", None),
        P("gx", "gy", None),
        P("gx", "gy", None),
        P("gx", "gy", None),
        P("gx", "gy"),
    )
    out_specs = (P(None, "gx", "gy", None), P(None, "gx", "gy", None))
    return jax.shard_map(
        per_device, mesh=mesh, in_specs=in_specs, out_specs=out_specs, check_vma=False
    )
```

```python
import jax
import jax.numpy as jnp
from jax import lax
from jax.sharding import PartitionSpec as P
from jax.experimental import pallas as pl
from jax.experimental.pallas import tpu as pltpu

TILE = 8
COARSE = 2
SUBSTEPS = 4


def level_scale(exponent):
    return jnp.where(exponent == 2, 0.25, jnp.where(exponent == 1, 0.5, 1.0)).astype(jnp.float32)


def centre(field):
    return field[1:-1, 1:-1]


def plus_x(field):
    return field[2:, 1:-1]


def minus_x(field):
    return field[:-2, 1:-1]


def plus_y(field):
    return field[1:-1, 2:]


def minus_y(field):
    return field[1:-1, :-2]


def z_forward(field):
    return jnp.concatenate([field[..., 1:], jnp.zeros_like(field[..., :1])], axis=-1) - field


def z_backward(field):
    return field - jnp.concatenate([jnp.zeros_like(field[..., :1]), field[..., :-1]], axis=-1)


def velocity_forces(padded, stress_zz):
    stress_xx, stress_yy, stress_xy, stress_xz, stress_yz = (
        padded[0],
        padded[1],
        padded[2],
        padded[3],
        padded[4],
    )
    force_x = (
        plus_x(stress_xx)
        - centre(stress_xx)
        + (centre(stress_xy) - minus_y(stress_xy))
        + z_backward(centre(stress_xz))
    )
    force_y = (
        centre(stress_xy)
        - minus_x(stress_xy)
        + (plus_y(stress_yy) - centre(stress_yy))
        + z_backward(centre(stress_yz))
    )
    force_z = (
        centre(stress_xz)
        - minus_x(stress_xz)
        + (centre(stress_yz) - minus_y(stress_yz))
        + z_forward(stress_zz)
    )
    return jnp.stack([force_x, force_y, force_z])


def advance_velocity(velocity, forces, push_coef, active):
    fresh = velocity + push_coef * forces
    if active is None:
        return fresh
    return jnp.where(active, fresh, velocity)


def advance_stress(stress, vel_padded, lam_coef, shear_coef, active):
    vel_x, vel_y, vel_z = (vel_padded[0], vel_padded[1], vel_padded[2])
    strain_x = centre(vel_x) - minus_x(vel_x)
    strain_y = centre(vel_y) - minus_y(vel_y)
    strain_z = z_backward(centre(vel_z))
    shear_xy = plus_y(vel_x) - centre(vel_x) + (plus_x(vel_y) - centre(vel_y))
    shear_xz = z_forward(centre(vel_x)) + (plus_x(vel_z) - centre(vel_z))
    shear_yz = z_forward(centre(vel_y)) + (plus_y(vel_z) - centre(vel_z))
    trace_sum = strain_x + strain_y + strain_z
    two_shear = 2.0 * shear_coef
    fresh = jnp.stack(
        [
            stress[0] + (lam_coef * trace_sum + two_shear * strain_x),
            stress[1] + (lam_coef * trace_sum + two_shear * strain_y),
            stress[2] + shear_coef * shear_xy,
            stress[3] + shear_coef * shear_xz,
            stress[4] + shear_coef * shear_yz,
            stress[5] + (lam_coef * trace_sum + two_shear * strain_z),
        ]
    )
    if active is None:
        return fresh
    return jnp.where(active, fresh, stress)


def with_blocks(cells, axis, dim):
    count = lax.axis_size(axis)
    from_below = lax.ppermute(cells, axis, [(i, i + 1) for i in range(count - 1)])
    from_above = lax.ppermute(cells, axis, [(i + 1, i) for i in range(count - 1)])
    return jnp.concatenate([from_below, cells, from_above], axis=dim)


INTERPRET = False
YOFF = 8


def lane_shifts(shape):
    axis = len(shape) - 1
    width = shape[-1]
    lane = lax.broadcasted_iota(jnp.int32, shape, axis)
    first = lane == 0
    last = lane == width - 1

    def z_backward(f):
        return f - jnp.where(first, 0.0, pltpu.roll(f, 1, axis))

    def z_forward(f):
        return jnp.where(last, 0.0, pltpu.roll(f, width - 1, axis)) - f

    return z_backward, z_forward


def substeps_kernel(below_ref, mid_ref, above_ref, vel_out, strs_out, vbuf, sbuf, cbuf, sems):
    piece = mid_ref.shape[1]
    rows, cols, depth = 3 * piece, mid_ref.shape[2], mid_ref.shape[3]
    ny = vel_out.shape[2]
    nx = vel_out.shape[1]
    halo = (rows - nx) // 2
    pad_rows = vbuf.shape[2] - cols - YOFF
    copies = []
    for k, src in enumerate((below_ref, mid_ref, above_ref)):
        at = 1 + k * piece
        targets = (
            (src.at[0:3], vbuf.at[:, at : at + piece, YOFF : YOFF + cols, :]),
            (src.at[3:9], sbuf.at[:, at : at + piece, YOFF : YOFF + cols, :]),
            (src.at[9:12], cbuf.at[:, at - 1 : at - 1 + piece, :, :]),
        )
        for src_view, dst_view in targets:
            copy = pltpu.make_async_copy(src_view, dst_view, sems.at[len(copies)])
            copy.start()
            copies.append(copy)
    zero_y = jnp.zeros((vbuf.shape[1], YOFF, depth), jnp.float32)
    zero_y2 = jnp.zeros((vbuf.shape[1], pad_rows, depth), jnp.float32)
    zero_x = jnp.zeros((1, cols, depth), jnp.float32)
    for buf, count in ((vbuf, 3), (sbuf, 6)):
        for c in range(count):
            buf[c, :, 0:YOFF, :] = zero_y
            buf[c, :, YOFF + cols :, :] = zero_y2
            buf[c, 0:1, YOFF : YOFF + cols, :] = zero_x
            buf[c, rows + 1 : rows + 2, YOFF : YOFF + cols, :] = zero_x
    for copy in copies:
        copy.wait()
    z_backward, z_forward = lane_shifts((1, cols, depth))
    ys = pl.ds(YOFF, cols)
    ym = pl.ds(YOFF - 1, cols)
    yp = pl.ds(YOFF + 1, cols)

    def mask_of(sub, r):
        if sub == 3:
            return None
        field = 10 if sub == 1 else 11
        return cbuf[field - 9, pl.ds(r, 1), :, :] < 0.0

    def keep(active, fresh, old):
        return fresh if active is None else jnp.where(active, fresh, old)

    for step in range(COARSE):
        for sub in range(SUBSTEPS):
            t = step * SUBSTEPS + sub
            lo, hi = t + 1, rows + 1 - t

            def vel_row(b, carry, sub=sub):
                r = b - 1
                sxx_c = sbuf[0, pl.ds(b, 1), ys, :]
                sxx_px = sbuf[0, pl.ds(b + 1, 1), ys, :]
                syy_c = sbuf[1, pl.ds(b, 1), ys, :]
                syy_py = sbuf[1, pl.ds(b, 1), yp, :]
                sxy_c = sbuf[2, pl.ds(b, 1), ys, :]
                sxy_my = sbuf[2, pl.ds(b, 1), ym, :]
                sxy_mx = sbuf[2, pl.ds(b - 1, 1), ys, :]
                sxz_c = sbuf[3, pl.ds(b, 1), ys, :]
                sxz_mx = sbuf[3, pl.ds(b - 1, 1), ys, :]
                syz_c = sbuf[4, pl.ds(b, 1), ys, :]
                syz_my = sbuf[4, pl.ds(b, 1), ym, :]
                szz_c = sbuf[5, pl.ds(b, 1), ys, :]
                force_x = sxx_px - sxx_c + (sxy_c - sxy_my) + z_backward(sxz_c)
                force_y = sxy_c - sxy_mx + (syy_py - syy_c) + z_backward(syz_c)
                force_z = sxz_c - sxz_mx + (syz_c - syz_my) + z_forward(szz_c)
                push = cbuf[0, pl.ds(r, 1), :, :]
                active = mask_of(sub, r)
                for c, force in enumerate((force_x, force_y, force_z)):
                    old = vbuf[c, pl.ds(b, 1), ys, :]
                    vbuf[c, pl.ds(b, 1), ys, :] = keep(active, old + push * force, old)
                return carry

            lax.fori_loop(lo, hi, vel_row, 0, unroll=True)

            def strs_row(b, carry, sub=sub):
                r = b - 1
                vx_c = vbuf[0, pl.ds(b, 1), ys, :]
                vx_mx = vbuf[0, pl.ds(b - 1, 1), ys, :]
                vx_py = vbuf[0, pl.ds(b, 1), yp, :]
                vy_c = vbuf[1, pl.ds(b, 1), ys, :]
                vy_my = vbuf[1, pl.ds(b, 1), ym, :]
                vy_px = vbuf[1, pl.ds(b + 1, 1), ys, :]
                vz_c = vbuf[2, pl.ds(b, 1), ys, :]
                vz_px = vbuf[2, pl.ds(b + 1, 1), ys, :]
                vz_py = vbuf[2, pl.ds(b, 1), yp, :]
                strain_x = vx_c - vx_mx
                strain_y = vy_c - vy_my
                strain_z = z_backward(vz_c)
                shear_xy = vx_py - vx_c + (vy_px - vy_c)
                shear_xz = z_forward(vx_c) + (vz_px - vz_c)
                shear_yz = z_forward(vy_c) + (vz_py - vz_c)
                trace_sum = strain_x + strain_y + strain_z
                lam = jnp.abs(cbuf[1, pl.ds(r, 1), :, :])
                shear = jnp.abs(cbuf[2, pl.ds(r, 1), :, :])
                two_shear = 2.0 * shear
                adds = (
                    lam * trace_sum + two_shear * strain_x,
                    lam * trace_sum + two_shear * strain_y,
                    shear * shear_xy,
                    shear * shear_xz,
                    shear * shear_yz,
                    lam * trace_sum + two_shear * strain_z,
                )
                active = mask_of(sub, r)
                for c, add in enumerate(adds):
                    old = sbuf[c, pl.ds(b, 1), ys, :]
                    sbuf[c, pl.ds(b, 1), ys, :] = keep(active, old + add, old)
                return carry

            lax.fori_loop(lo, hi, strs_row, 0, unroll=True)

    xs = slice(halo + 1, halo + 1 + nx)
    yc = slice(YOFF + halo, YOFF + halo + ny)
    for c in range(3):
        vel_out[c] = vbuf[c, xs, yc, :]
    for c in range(6):
        strs_out[c] = sbuf[c, xs, yc, :]


def substeps(below, mid, above, nx, ny):
    fields, piece, cols, depth = mid.shape
    rows = 3 * piece
    return pl.pallas_call(
        substeps_kernel,
        out_shape=(
            jax.ShapeDtypeStruct((3, nx, ny, depth), jnp.float32),
            jax.ShapeDtypeStruct((6, nx, ny, depth), jnp.float32),
        ),
        scratch_shapes=[
            pltpu.VMEM((3, rows + 2, cols + 2 * YOFF, depth), jnp.float32),
            pltpu.VMEM((6, rows + 2, cols + 2 * YOFF, depth), jnp.float32),
            pltpu.VMEM((fields - 9, rows, cols, depth), jnp.float32),
            pltpu.SemaphoreType.DMA((9,)),
        ],
        in_specs=[pl.BlockSpec(memory_space=pl.ANY)] * 3,
        interpret=INTERPRET,
    )(below, mid, above)


def pack_kernel(e_ref, v_ref, s_ref, b_ref, l_ref, m_ref, out_ref):
    e = e_ref[0, 0]
    scale = jnp.where(e == 2, 0.25, jnp.where(e == 1, 0.5, 1.0)).astype(jnp.float32)
    lam_sign = jnp.where(e >= 1, -1.0, 1.0).astype(jnp.float32)
    shear_sign = jnp.where(e == 2, -1.0, 1.0).astype(jnp.float32)
    for c in range(3):
        out_ref[c] = v_ref[c]
    for c in range(6):
        out_ref[3 + c] = s_ref[c]
    out_ref[9] = b_ref[...] * scale
    out_ref[10] = (l_ref[...] * scale) * lam_sign
    out_ref[11] = (m_ref[...] * scale) * shear_sign


def pack(velocity, stress, buoyancy, lame_lambda, lame_mu, rate_exponent):
    nx, ny, depth = buoyancy.shape
    vmem = pl.BlockSpec(memory_space=pltpu.VMEM)
    return pl.pallas_call(
        pack_kernel,
        out_shape=jax.ShapeDtypeStruct((12, nx, ny, depth), jnp.float32),
        in_specs=[pl.BlockSpec(memory_space=pltpu.SMEM)] + [vmem] * 5,
        out_specs=vmem,
        interpret=INTERPRET,
    )(rate_exponent, velocity, stress, buoyancy, lame_lambda, lame_mu)


def per_device(velocity, stress, buoyancy, lame_lambda, lame_mu, rate_exponent):
    nx, ny = velocity.shape[1], velocity.shape[2]
    block = pack(velocity, stress, buoyancy, lame_lambda, lame_mu, rate_exponent)
    block = with_blocks(block, "gy", 2)
    count = lax.axis_size("gx")
    below = lax.ppermute(block, "gx", [(i, i + 1) for i in range(count - 1)])
    above = lax.ppermute(block, "gx", [(i + 1, i) for i in range(count - 1)])
    return substeps(below, block, above, nx, ny)


def solution(mesh):
    in_specs = (
        P(None, "gx", "gy", None),
        P(None, "gx", "gy", None),
        P("gx", "gy", None),
        P("gx", "gy", None),
        P("gx", "gy", None),
        P("gx", "gy"),
    )
    out_specs = (P(None, "gx", "gy", None), P(None, "gx", "gy", None))
    return jax.shard_map(
        per_device, mesh=mesh, in_specs=in_specs, out_specs=out_specs, check_vma=False
    )
```

```python
import jax
import jax.numpy as jnp
from jax import lax
from jax.sharding import PartitionSpec as P
from jax.experimental import pallas as pl
from jax.experimental.pallas import tpu as pltpu

TILE = 8
COARSE = 2
SUBSTEPS = 4


def level_scale(exponent):
    return jnp.where(exponent == 2, 0.25, jnp.where(exponent == 1, 0.5, 1.0)).astype(jnp.float32)


def centre(field):
    return field[1:-1, 1:-1]


def plus_x(field):
    return field[2:, 1:-1]


def minus_x(field):
    return field[:-2, 1:-1]


def plus_y(field):
    return field[1:-1, 2:]


def minus_y(field):
    return field[1:-1, :-2]


def z_forward(field):
    return jnp.concatenate([field[..., 1:], jnp.zeros_like(field[..., :1])], axis=-1) - field


def z_backward(field):
    return field - jnp.concatenate([jnp.zeros_like(field[..., :1]), field[..., :-1]], axis=-1)


def velocity_forces(padded, stress_zz):
    stress_xx, stress_yy, stress_xy, stress_xz, stress_yz = (
        padded[0],
        padded[1],
        padded[2],
        padded[3],
        padded[4],
    )
    force_x = (
        plus_x(stress_xx)
        - centre(stress_xx)
        + (centre(stress_xy) - minus_y(stress_xy))
        + z_backward(centre(stress_xz))
    )
    force_y = (
        centre(stress_xy)
        - minus_x(stress_xy)
        + (plus_y(stress_yy) - centre(stress_yy))
        + z_backward(centre(stress_yz))
    )
    force_z = (
        centre(stress_xz)
        - minus_x(stress_xz)
        + (centre(stress_yz) - minus_y(stress_yz))
        + z_forward(stress_zz)
    )
    return jnp.stack([force_x, force_y, force_z])


def advance_velocity(velocity, forces, push_coef, active):
    fresh = velocity + push_coef * forces
    if active is None:
        return fresh
    return jnp.where(active, fresh, velocity)


def advance_stress(stress, vel_padded, lam_coef, shear_coef, active):
    vel_x, vel_y, vel_z = (vel_padded[0], vel_padded[1], vel_padded[2])
    strain_x = centre(vel_x) - minus_x(vel_x)
    strain_y = centre(vel_y) - minus_y(vel_y)
    strain_z = z_backward(centre(vel_z))
    shear_xy = plus_y(vel_x) - centre(vel_x) + (plus_x(vel_y) - centre(vel_y))
    shear_xz = z_forward(centre(vel_x)) + (plus_x(vel_z) - centre(vel_z))
    shear_yz = z_forward(centre(vel_y)) + (plus_y(vel_z) - centre(vel_z))
    trace_sum = strain_x + strain_y + strain_z
    two_shear = 2.0 * shear_coef
    fresh = jnp.stack(
        [
            stress[0] + (lam_coef * trace_sum + two_shear * strain_x),
            stress[1] + (lam_coef * trace_sum + two_shear * strain_y),
            stress[2] + shear_coef * shear_xy,
            stress[3] + shear_coef * shear_xz,
            stress[4] + shear_coef * shear_yz,
            stress[5] + (lam_coef * trace_sum + two_shear * strain_z),
        ]
    )
    if active is None:
        return fresh
    return jnp.where(active, fresh, stress)


def with_blocks(cells, axis, dim):
    count = lax.axis_size(axis)
    from_below = lax.ppermute(cells, axis, [(i, i + 1) for i in range(count - 1)])
    from_above = lax.ppermute(cells, axis, [(i + 1, i) for i in range(count - 1)])
    return jnp.concatenate([from_below, cells, from_above], axis=dim)


INTERPRET = False
YOFF = 8


def lane_shifts(shape):
    axis = len(shape) - 1
    width = shape[-1]
    lane = lax.broadcasted_iota(jnp.int32, shape, axis)
    first = lane == 0
    last = lane == width - 1

    def z_backward(f):
        return f - jnp.where(first, 0.0, pltpu.roll(f, 1, axis))

    def z_forward(f):
        return jnp.where(last, 0.0, pltpu.roll(f, width - 1, axis)) - f

    return z_backward, z_forward


def substeps_kernel(below_ref, mid_ref, above_ref, vel_out, strs_out, vbuf, sbuf, cbuf, sems):
    piece = mid_ref.shape[1]
    rows, cols, depth = 3 * piece, mid_ref.shape[2], mid_ref.shape[3]
    ny = vel_out.shape[2]
    nx = vel_out.shape[1]
    halo = (rows - nx) // 2
    pad_rows = vbuf.shape[2] - cols - YOFF
    copies = []
    for k, src in enumerate((below_ref, mid_ref, above_ref)):
        at = 1 + k * piece
        targets = (
            (src.at[0:3], vbuf.at[:, at : at + piece, YOFF : YOFF + cols, :]),
            (src.at[3:9], sbuf.at[:, at : at + piece, YOFF : YOFF + cols, :]),
            (src.at[9:12], cbuf.at[:, at - 1 : at - 1 + piece, :, :]),
        )
        for src_view, dst_view in targets:
            copy = pltpu.make_async_copy(src_view, dst_view, sems.at[len(copies)])
            copy.start()
            copies.append(copy)
    zero_y = jnp.zeros((vbuf.shape[1], YOFF, depth), jnp.float32)
    zero_y2 = jnp.zeros((vbuf.shape[1], pad_rows, depth), jnp.float32)
    zero_x = jnp.zeros((1, cols, depth), jnp.float32)
    for buf, count in ((vbuf, 3), (sbuf, 6)):
        for c in range(count):
            buf[c, :, 0:YOFF, :] = zero_y
            buf[c, :, YOFF + cols :, :] = zero_y2
            buf[c, 0:1, YOFF : YOFF + cols, :] = zero_x
            buf[c, rows + 1 : rows + 2, YOFF : YOFF + cols, :] = zero_x
    for copy in copies:
        copy.wait()
    z_backward, z_forward = lane_shifts((1, cols, depth))
    ys = pl.ds(YOFF, cols)
    ym = pl.ds(YOFF - 1, cols)
    yp = pl.ds(YOFF + 1, cols)

    def mask_of(sub, r):
        if sub == 3:
            return None
        field = 10 if sub == 1 else 11
        return cbuf[field - 9, pl.ds(r, 1), :, :] < 0.0

    def keep(active, fresh, old):
        return fresh if active is None else jnp.where(active, fresh, old)

    for step in range(COARSE):
        for sub in range(SUBSTEPS):
            t = step * SUBSTEPS + sub
            lo, hi = t + 1, rows + 1 - t

            def vel_row(b, carry, sub=sub):
                r = b - 1
                sxx_c = sbuf[0, pl.ds(b, 1), ys, :]
                sxx_px = sbuf[0, pl.ds(b + 1, 1), ys, :]
                syy_c = sbuf[1, pl.ds(b, 1), ys, :]
                syy_py = sbuf[1, pl.ds(b, 1), yp, :]
                sxy_c = sbuf[2, pl.ds(b, 1), ys, :]
                sxy_my = sbuf[2, pl.ds(b, 1), ym, :]
                sxy_mx = sbuf[2, pl.ds(b - 1, 1), ys, :]
                sxz_c = sbuf[3, pl.ds(b, 1), ys, :]
                sxz_mx = sbuf[3, pl.ds(b - 1, 1), ys, :]
                syz_c = sbuf[4, pl.ds(b, 1), ys, :]
                syz_my = sbuf[4, pl.ds(b, 1), ym, :]
                szz_c = sbuf[5, pl.ds(b, 1), ys, :]
                force_x = sxx_px - sxx_c + (sxy_c - sxy_my) + z_backward(sxz_c)
                force_y = sxy_c - sxy_mx + (syy_py - syy_c) + z_backward(syz_c)
                force_z = sxz_c - sxz_mx + (syz_c - syz_my) + z_forward(szz_c)
                push = cbuf[0, pl.ds(r, 1), :, :]
                active = mask_of(sub, r)
                for c, force in enumerate((force_x, force_y, force_z)):
                    old = vbuf[c, pl.ds(b, 1), ys, :]
                    vbuf[c, pl.ds(b, 1), ys, :] = keep(active, old + push * force, old)
                return carry

            lax.fori_loop(lo, hi, vel_row, 0, unroll=True)

            def strs_row(b, carry, sub=sub):
                r = b - 1
                vx_c = vbuf[0, pl.ds(b, 1), ys, :]
                vx_mx = vbuf[0, pl.ds(b - 1, 1), ys, :]
                vx_py = vbuf[0, pl.ds(b, 1), yp, :]
                vy_c = vbuf[1, pl.ds(b, 1), ys, :]
                vy_my = vbuf[1, pl.ds(b, 1), ym, :]
                vy_px = vbuf[1, pl.ds(b + 1, 1), ys, :]
                vz_c = vbuf[2, pl.ds(b, 1), ys, :]
                vz_px = vbuf[2, pl.ds(b + 1, 1), ys, :]
                vz_py = vbuf[2, pl.ds(b, 1), yp, :]
                strain_x = vx_c - vx_mx
                strain_y = vy_c - vy_my
                strain_z = z_backward(vz_c)
                shear_xy = vx_py - vx_c + (vy_px - vy_c)
                shear_xz = z_forward(vx_c) + (vz_px - vz_c)
                shear_yz = z_forward(vy_c) + (vz_py - vz_c)
                trace_sum = strain_x + strain_y + strain_z
                lam = jnp.abs(cbuf[1, pl.ds(r, 1), :, :])
                shear = jnp.abs(cbuf[2, pl.ds(r, 1), :, :])
                two_shear = 2.0 * shear
                adds = (
                    lam * trace_sum + two_shear * strain_x,
                    lam * trace_sum + two_shear * strain_y,
                    shear * shear_xy,
                    shear * shear_xz,
                    shear * shear_yz,
                    lam * trace_sum + two_shear * strain_z,
                )
                active = mask_of(sub, r)
                for c, add in enumerate(adds):
                    old = sbuf[c, pl.ds(b, 1), ys, :]
                    sbuf[c, pl.ds(b, 1), ys, :] = keep(active, old + add, old)
                return carry

            lax.fori_loop(lo + 1, hi - 1, strs_row, 0, unroll=True)

    xs = slice(halo + 1, halo + 1 + nx)
    yc = slice(YOFF + halo, YOFF + halo + ny)
    for c in range(3):
        vel_out[c] = vbuf[c, xs, yc, :]
    for c in range(6):
        strs_out[c] = sbuf[c, xs, yc, :]


def substeps(below, mid, above, nx, ny):
    fields, piece, cols, depth = mid.shape
    rows = 3 * piece
    return pl.pallas_call(
        substeps_kernel,
        out_shape=(
            jax.ShapeDtypeStruct((3, nx, ny, depth), jnp.float32),
            jax.ShapeDtypeStruct((6, nx, ny, depth), jnp.float32),
        ),
        scratch_shapes=[
            pltpu.VMEM((3, rows + 2, cols + 2 * YOFF, depth), jnp.float32),
            pltpu.VMEM((6, rows + 2, cols + 2 * YOFF, depth), jnp.float32),
            pltpu.VMEM((fields - 9, rows, cols, depth), jnp.float32),
            pltpu.SemaphoreType.DMA((9,)),
        ],
        in_specs=[pl.BlockSpec(memory_space=pl.ANY)] * 3,
        interpret=INTERPRET,
    )(below, mid, above)


def pack_kernel(e_ref, v_ref, s_ref, b_ref, l_ref, m_ref, out_ref):
    e = e_ref[0, 0]
    scale = jnp.where(e == 2, 0.25, jnp.where(e == 1, 0.5, 1.0)).astype(jnp.float32)
    lam_sign = jnp.where(e >= 1, -1.0, 1.0).astype(jnp.float32)
    shear_sign = jnp.where(e == 2, -1.0, 1.0).astype(jnp.float32)
    for c in range(3):
        out_ref[c] = v_ref[c]
    for c in range(6):
        out_ref[3 + c] = s_ref[c]
    out_ref[9] = b_ref[...] * scale
    out_ref[10] = (l_ref[...] * scale) * lam_sign
    out_ref[11] = (m_ref[...] * scale) * shear_sign


def pack(velocity, stress, buoyancy, lame_lambda, lame_mu, rate_exponent):
    nx, ny, depth = buoyancy.shape
    vmem = pl.BlockSpec(memory_space=pltpu.VMEM)
    return pl.pallas_call(
        pack_kernel,
        out_shape=jax.ShapeDtypeStruct((12, nx, ny, depth), jnp.float32),
        in_specs=[pl.BlockSpec(memory_space=pltpu.SMEM)] + [vmem] * 5,
        out_specs=vmem,
        interpret=INTERPRET,
    )(rate_exponent, velocity, stress, buoyancy, lame_lambda, lame_mu)


def per_device(velocity, stress, buoyancy, lame_lambda, lame_mu, rate_exponent):
    nx, ny = velocity.shape[1], velocity.shape[2]
    block = pack(velocity, stress, buoyancy, lame_lambda, lame_mu, rate_exponent)
    block = with_blocks(block, "gy", 2)
    count = lax.axis_size("gx")
    below = lax.ppermute(block, "gx", [(i, i + 1) for i in range(count - 1)])
    above = lax.ppermute(block, "gx", [(i + 1, i) for i in range(count - 1)])
    return substeps(below, block, above, nx, ny)


def solution(mesh):
    in_specs = (
        P(None, "gx", "gy", None),
        P(None, "gx", "gy", None),
        P("gx", "gy", None),
        P("gx", "gy", None),
        P("gx", "gy", None),
        P("gx", "gy"),
    )
    out_specs = (P(None, "gx", "gy", None), P(None, "gx", "gy", None))
    return jax.shard_map(
        per_device, mesh=mesh, in_specs=in_specs, out_specs=out_specs, check_vma=False
    )
```

```python
import jax
import jax.numpy as jnp
from jax import lax
from jax.sharding import PartitionSpec as P
from jax.experimental import pallas as pl
from jax.experimental.pallas import tpu as pltpu

TILE = 8
COARSE = 2
SUBSTEPS = 4


def level_scale(exponent):
    return jnp.where(exponent == 2, 0.25, jnp.where(exponent == 1, 0.5, 1.0)).astype(jnp.float32)


def centre(field):
    return field[1:-1, 1:-1]


def plus_x(field):
    return field[2:, 1:-1]


def minus_x(field):
    return field[:-2, 1:-1]


def plus_y(field):
    return field[1:-1, 2:]


def minus_y(field):
    return field[1:-1, :-2]


def z_forward(field):
    return jnp.concatenate([field[..., 1:], jnp.zeros_like(field[..., :1])], axis=-1) - field


def z_backward(field):
    return field - jnp.concatenate([jnp.zeros_like(field[..., :1]), field[..., :-1]], axis=-1)


def velocity_forces(padded, stress_zz):
    stress_xx, stress_yy, stress_xy, stress_xz, stress_yz = (
        padded[0],
        padded[1],
        padded[2],
        padded[3],
        padded[4],
    )
    force_x = (
        plus_x(stress_xx)
        - centre(stress_xx)
        + (centre(stress_xy) - minus_y(stress_xy))
        + z_backward(centre(stress_xz))
    )
    force_y = (
        centre(stress_xy)
        - minus_x(stress_xy)
        + (plus_y(stress_yy) - centre(stress_yy))
        + z_backward(centre(stress_yz))
    )
    force_z = (
        centre(stress_xz)
        - minus_x(stress_xz)
        + (centre(stress_yz) - minus_y(stress_yz))
        + z_forward(stress_zz)
    )
    return jnp.stack([force_x, force_y, force_z])


def advance_velocity(velocity, forces, push_coef, active):
    fresh = velocity + push_coef * forces
    if active is None:
        return fresh
    return jnp.where(active, fresh, velocity)


def advance_stress(stress, vel_padded, lam_coef, shear_coef, active):
    vel_x, vel_y, vel_z = (vel_padded[0], vel_padded[1], vel_padded[2])
    strain_x = centre(vel_x) - minus_x(vel_x)
    strain_y = centre(vel_y) - minus_y(vel_y)
    strain_z = z_backward(centre(vel_z))
    shear_xy = plus_y(vel_x) - centre(vel_x) + (plus_x(vel_y) - centre(vel_y))
    shear_xz = z_forward(centre(vel_x)) + (plus_x(vel_z) - centre(vel_z))
    shear_yz = z_forward(centre(vel_y)) + (plus_y(vel_z) - centre(vel_z))
    trace_sum = strain_x + strain_y + strain_z
    two_shear = 2.0 * shear_coef
    fresh = jnp.stack(
        [
            stress[0] + (lam_coef * trace_sum + two_shear * strain_x),
            stress[1] + (lam_coef * trace_sum + two_shear * strain_y),
            stress[2] + shear_coef * shear_xy,
            stress[3] + shear_coef * shear_xz,
            stress[4] + shear_coef * shear_yz,
            stress[5] + (lam_coef * trace_sum + two_shear * strain_z),
        ]
    )
    if active is None:
        return fresh
    return jnp.where(active, fresh, stress)


def with_blocks(cells, axis, dim):
    count = lax.axis_size(axis)
    from_below = lax.ppermute(cells, axis, [(i, i + 1) for i in range(count - 1)])
    from_above = lax.ppermute(cells, axis, [(i + 1, i) for i in range(count - 1)])
    return jnp.concatenate([from_below, cells, from_above], axis=dim)


INTERPRET = False
YOFF = 8


def lane_shifts(shape):
    axis = len(shape) - 1
    width = shape[-1]
    lane = lax.broadcasted_iota(jnp.int32, shape, axis)
    first = lane == 0
    last = lane == width - 1

    def z_backward(f):
        return f - jnp.where(first, 0.0, pltpu.roll(f, 1, axis))

    def z_forward(f):
        return jnp.where(last, 0.0, pltpu.roll(f, width - 1, axis)) - f

    return z_backward, z_forward


def substeps_kernel(below_ref, mid_ref, above_ref, vel_out, strs_out, vbuf, sbuf, cbuf, sems):
    piece = mid_ref.shape[1]
    rows, cols, depth = 3 * piece, mid_ref.shape[2], mid_ref.shape[3]
    ny = vel_out.shape[2]
    nx = vel_out.shape[1]
    halo = (rows - nx) // 2
    pad_rows = vbuf.shape[2] - cols - YOFF
    copies = []
    for k, src in enumerate((below_ref, mid_ref, above_ref)):
        at = 1 + k * piece
        targets = (
            (src.at[0:3], vbuf.at[:, at : at + piece, YOFF : YOFF + cols, :]),
            (src.at[3:9], sbuf.at[:, at : at + piece, YOFF : YOFF + cols, :]),
            (src.at[9:12], cbuf.at[:, at - 1 : at - 1 + piece, :, :]),
        )
        for src_view, dst_view in targets:
            copy = pltpu.make_async_copy(src_view, dst_view, sems.at[len(copies)])
            copy.start()
            copies.append(copy)
    zero_y = jnp.zeros((vbuf.shape[1], YOFF, depth), jnp.float32)
    zero_y2 = jnp.zeros((vbuf.shape[1], pad_rows, depth), jnp.float32)
    zero_x = jnp.zeros((1, cols, depth), jnp.float32)
    for buf, count in ((vbuf, 3), (sbuf, 6)):
        for c in range(count):
            buf[c, :, 0:YOFF, :] = zero_y
            buf[c, :, YOFF + cols :, :] = zero_y2
            buf[c, 0:1, YOFF : YOFF + cols, :] = zero_x
            buf[c, rows + 1 : rows + 2, YOFF : YOFF + cols, :] = zero_x
    for copy in copies:
        copy.wait()
    z_backward, z_forward = lane_shifts((1, cols, depth))
    ys = pl.ds(YOFF, cols)
    ym = pl.ds(YOFF - 1, cols)
    yp = pl.ds(YOFF + 1, cols)

    def mask_of(sub, r):
        if sub == 3:
            return None
        field = 10 if sub == 1 else 11
        return cbuf[field - 9, pl.ds(r, 1), :, :] < 0.0

    def keep(active, fresh, old):
        return fresh if active is None else jnp.where(active, fresh, old)

    for step in range(COARSE):
        for sub in range(SUBSTEPS):
            t = step * SUBSTEPS + sub
            lo, hi = t + 1, rows + 1 - t

            def vel_row(b, carry, sub=sub, comps=(0, 1, 2)):
                r = b - 1
                sxx_c = sbuf[0, pl.ds(b, 1), ys, :]
                sxx_px = sbuf[0, pl.ds(b + 1, 1), ys, :]
                syy_c = sbuf[1, pl.ds(b, 1), ys, :]
                syy_py = sbuf[1, pl.ds(b, 1), yp, :]
                sxy_c = sbuf[2, pl.ds(b, 1), ys, :]
                sxy_my = sbuf[2, pl.ds(b, 1), ym, :]
                sxy_mx = sbuf[2, pl.ds(b - 1, 1), ys, :]
                sxz_c = sbuf[3, pl.ds(b, 1), ys, :]
                sxz_mx = sbuf[3, pl.ds(b - 1, 1), ys, :]
                syz_c = sbuf[4, pl.ds(b, 1), ys, :]
                syz_my = sbuf[4, pl.ds(b, 1), ym, :]
                szz_c = sbuf[5, pl.ds(b, 1), ys, :]
                force_x = sxx_px - sxx_c + (sxy_c - sxy_my) + z_backward(sxz_c)
                force_y = sxy_c - sxy_mx + (syy_py - syy_c) + z_backward(syz_c)
                force_z = sxz_c - sxz_mx + (syz_c - syz_my) + z_forward(szz_c)
                push = cbuf[0, pl.ds(r, 1), :, :]
                active = mask_of(sub, r)
                for c, force in enumerate((force_x, force_y, force_z)):
                    if c not in comps:
                        continue
                    old = vbuf[c, pl.ds(b, 1), ys, :]
                    vbuf[c, pl.ds(b, 1), ys, :] = keep(active, old + push * force, old)
                return carry

            vel_row(lo, 0, comps=(0,))
            lax.fori_loop(lo + 1, hi - 1, vel_row, 0, unroll=True)
            vel_row(hi - 1, 0, comps=(1, 2))

            def strs_row(b, carry, sub=sub):
                r = b - 1
                vx_c = vbuf[0, pl.ds(b, 1), ys, :]
                vx_mx = vbuf[0, pl.ds(b - 1, 1), ys, :]
                vx_py = vbuf[0, pl.ds(b, 1), yp, :]
                vy_c = vbuf[1, pl.ds(b, 1), ys, :]
                vy_my = vbuf[1, pl.ds(b, 1), ym, :]
                vy_px = vbuf[1, pl.ds(b + 1, 1), ys, :]
                vz_c = vbuf[2, pl.ds(b, 1), ys, :]
                vz_px = vbuf[2, pl.ds(b + 1, 1), ys, :]
                vz_py = vbuf[2, pl.ds(b, 1), yp, :]
                strain_x = vx_c - vx_mx
                strain_y = vy_c - vy_my
                strain_z = z_backward(vz_c)
                shear_xy = vx_py - vx_c + (vy_px - vy_c)
                shear_xz = z_forward(vx_c) + (vz_px - vz_c)
                shear_yz = z_forward(vy_c) + (vz_py - vz_c)
                trace_sum = strain_x + strain_y + strain_z
                lam = jnp.abs(cbuf[1, pl.ds(r, 1), :, :])
                shear = jnp.abs(cbuf[2, pl.ds(r, 1), :, :])
                two_shear = 2.0 * shear
                adds = (
                    lam * trace_sum + two_shear * strain_x,
                    lam * trace_sum + two_shear * strain_y,
                    shear * shear_xy,
                    shear * shear_xz,
                    shear * shear_yz,
                    lam * trace_sum + two_shear * strain_z,
                )
                active = mask_of(sub, r)
                for c, add in enumerate(adds):
                    old = sbuf[c, pl.ds(b, 1), ys, :]
                    sbuf[c, pl.ds(b, 1), ys, :] = keep(active, old + add, old)
                return carry

            lax.fori_loop(lo + 1, hi - 1, strs_row, 0, unroll=True)

    xs = slice(halo + 1, halo + 1 + nx)
    yc = slice(YOFF + halo, YOFF + halo + ny)
    for c in range(3):
        vel_out[c] = vbuf[c, xs, yc, :]
    for c in range(6):
        strs_out[c] = sbuf[c, xs, yc, :]


def substeps(below, mid, above, nx, ny):
    fields, piece, cols, depth = mid.shape
    rows = 3 * piece
    return pl.pallas_call(
        substeps_kernel,
        out_shape=(
            jax.ShapeDtypeStruct((3, nx, ny, depth), jnp.float32),
            jax.ShapeDtypeStruct((6, nx, ny, depth), jnp.float32),
        ),
        scratch_shapes=[
            pltpu.VMEM((3, rows + 2, cols + 2 * YOFF, depth), jnp.float32),
            pltpu.VMEM((6, rows + 2, cols + 2 * YOFF, depth), jnp.float32),
            pltpu.VMEM((fields - 9, rows, cols, depth), jnp.float32),
            pltpu.SemaphoreType.DMA((9,)),
        ],
        in_specs=[pl.BlockSpec(memory_space=pl.ANY)] * 3,
        interpret=INTERPRET,
    )(below, mid, above)


def pack_kernel(e_ref, v_ref, s_ref, b_ref, l_ref, m_ref, out_ref):
    e = e_ref[0, 0]
    scale = jnp.where(e == 2, 0.25, jnp.where(e == 1, 0.5, 1.0)).astype(jnp.float32)
    lam_sign = jnp.where(e >= 1, -1.0, 1.0).astype(jnp.float32)
    shear_sign = jnp.where(e == 2, -1.0, 1.0).astype(jnp.float32)
    for c in range(3):
        out_ref[c] = v_ref[c]
    for c in range(6):
        out_ref[3 + c] = s_ref[c]
    out_ref[9] = b_ref[...] * scale
    out_ref[10] = (l_ref[...] * scale) * lam_sign
    out_ref[11] = (m_ref[...] * scale) * shear_sign


def pack(velocity, stress, buoyancy, lame_lambda, lame_mu, rate_exponent):
    nx, ny, depth = buoyancy.shape
    vmem = pl.BlockSpec(memory_space=pltpu.VMEM)
    return pl.pallas_call(
        pack_kernel,
        out_shape=jax.ShapeDtypeStruct((12, nx, ny, depth), jnp.float32),
        in_specs=[pl.BlockSpec(memory_space=pltpu.SMEM)] + [vmem] * 5,
        out_specs=vmem,
        interpret=INTERPRET,
    )(rate_exponent, velocity, stress, buoyancy, lame_lambda, lame_mu)


def per_device(velocity, stress, buoyancy, lame_lambda, lame_mu, rate_exponent):
    nx, ny = velocity.shape[1], velocity.shape[2]
    block = pack(velocity, stress, buoyancy, lame_lambda, lame_mu, rate_exponent)
    block = with_blocks(block, "gy", 2)
    count = lax.axis_size("gx")
    below = lax.ppermute(block, "gx", [(i, i + 1) for i in range(count - 1)])
    above = lax.ppermute(block, "gx", [(i + 1, i) for i in range(count - 1)])
    return substeps(below, block, above, nx, ny)


def solution(mesh):
    in_specs = (
        P(None, "gx", "gy", None),
        P(None, "gx", "gy", None),
        P("gx", "gy", None),
        P("gx", "gy", None),
        P("gx", "gy", None),
        P("gx", "gy"),
    )
    out_specs = (P(None, "gx", "gy", None), P(None, "gx", "gy", None))
    return jax.shard_map(
        per_device, mesh=mesh, in_specs=in_specs, out_specs=out_specs, check_vma=False
    )
```
